32 devices in a mesh: ctx: 8 (over z, y), tp: 4 (over x, core).
Axes of the slice: x: 2, y: 2, z: 4, core: 2. Of those that a mesh axis runs over, the one named last changes fastest.
Arguments:
- tokens: bfloat16 [1024, 4096], P('ctx'), may hold values from -6 to 6
- w_query: bfloat16 [4096, 2048], P('ctx', 'tp'), may hold values from -0.09375 to 0.09375
- w_key: bfloat16 [4096, 2048], P('ctx', 'tp'), may hold values from -0.09375 to 0.09375
- w_value: bfloat16 [4096, 2048], P('ctx', 'tp'), may hold values from -0.09375 to 0.09375
- taps_query: float32 [3, 2048], P(None, 'tp'), may hold values from -3.5 to 3.5
- taps_key: float32 [3, 2048], P(None, 'tp'), may hold values from -3.5 to 3.5
- taps_value: float32 [3, 2048], P(None, 'tp'), may hold values from -3.5 to 3.5
- decay_rate: float32 [16, 2048], P(None, 'tp'), may hold values from 1e-05 to 0.03
- residue: float32 [16, 2048], P(None, 'tp'), may hold values from -1.5 to 1.5
- skip_gain: float32 [2048], P('tp'), may hold values from -3 to 3
- w_out: bfloat16 [2048, 4096], P('ctx', 'tp'), may hold values from -0.125 to 0.125
Outputs:
- layer_out: bfloat16 [1024, 4096], P('ctx', 'tp')
The draws below stay inside these ranges and needn't reach their ends.
All inputs are finite; a program needn't handle non-finite values.
Results may differ from the reference program's by a relative error of at most 0.015.
Values may be sent and summed in bfloat16 or wider, within the bound.
No kernel may reach another device: no remote copies, remote signals or barrier semaphores. Data moves between devices by JAX's collectives and lax.ppermute only.
A program may use at most 128 MiB of HBM per device.

```python
import math
import jax
import jax.numpy as jnp
from jax import lax

D = 4096
W = 2048
ORDER = 16
TOKENS = 1024


def block_levels(key, extent, cuts, least, high):
    gain = 1.0
    for axis_at, blocks in cuts:
        draws = jax.random.uniform(jax.random.fold_in(jax.random.fold_in(key, 6), axis_at), (blocks,), jnp.float32, least / len(cuts), high / len(cuts))
        gain = gain * jnp.repeat(jnp.exp(draws), extent[axis_at] // blocks).reshape((-1,) + (1,) * (len(extent) - 1 - axis_at))
    return gain


def gaussian(stream_key, extent, spread, most, shards=(), held_as=jnp.bfloat16):
    entries = spread * jax.random.normal(stream_key, extent, jnp.float32)
    if shards:
        entries = entries * block_levels(stream_key, extent, shards, -0.22, 0.18)
    return jnp.clip(entries, -most, most).astype(held_as)


def setup_inputs(seed: int = 0) -> dict:
    arg_keys = jax.random.split(jax.random.key(seed), 12)
    tokens = gaussian(arg_keys[0], (TOKENS, D), 1.0, 6.0, ((0, 8),))
    w_query = gaussian(arg_keys[1], (D, W), D ** -0.5, 0.09375, ((0, 8), (1, 4)))
    w_key = gaussian(arg_keys[2], (D, W), D ** -0.5, 0.09375, ((0, 8), (1, 4)))
    w_value = gaussian(arg_keys[3], (D, W), D ** -0.5, 0.09375, ((0, 8), (1, 4)))
    taps_query = gaussian(arg_keys[4], (3, W), 3 ** -0.5, 3.5, ((1, 4),), jnp.float32)
    taps_key = gaussian(arg_keys[5], (3, W), 3 ** -0.5, 3.5, ((1, 4),), jnp.float32)
    taps_value = gaussian(arg_keys[6], (3, W), 3 ** -0.5, 3.5, ((1, 4),), jnp.float32)
    decay_rate = jnp.clip(jnp.exp(math.log(0.03) - 8.006368 * jax.random.uniform(arg_keys[7], (ORDER, W), jnp.float32) ** block_levels(arg_keys[7], (ORDER, W), ((1, 4),), -0.2, 0.2)), 9.999999747378752e-06, 0.03)
    residue = gaussian(arg_keys[8], (ORDER, W), 0.25, 1.5, ((1, 4),), jnp.float32)
    skip_gain = gaussian(arg_keys[9], (W,), 0.5, 3.0, ((0, 4),), jnp.float32)
    w_out = gaussian(arg_keys[10], (W, D), W ** -0.5, 0.125, ((0, 8), (1, 4)))
    return dict(tokens=tokens, w_query=w_query, w_key=w_key, w_value=w_value, taps_query=taps_query, taps_key=taps_key, taps_value=taps_value, decay_rate=decay_rate, residue=residue, skip_gain=skip_gain, w_out=w_out)


def short_conv(signal, taps):
    padded = jnp.pad(signal, ((2, 0), (0, 0)))
    return taps[0] * padded[2:] + taps[1] * padded[1:-1] + taps[2] * padded[:-2]

def long_block(items):
    signal, rates, residues, skips = items
    length = signal.shape[0]
    times = jnp.arange(length, dtype=jnp.float32)
    coefs = residues * jnp.sqrt(2.0 * rates)
    kernel = jnp.zeros(signal.shape, jnp.float32)
    for mode in range(ORDER):
        kernel = kernel + coefs[mode] * jnp.exp(-rates[mode] * times[:, None])
    spectrum = jnp.fft.rfft(signal, n=2 * length, axis=0) * jnp.fft.rfft(kernel, n=2 * length, axis=0)
    convolved = jnp.fft.irfft(spectrum, n=2 * length, axis=0)[:length]
    return convolved + skips * signal

def reference(tokens, w_query, w_key, w_value, taps_query, taps_key, taps_value, decay_rate, residue, skip_gain, w_out):
    queries = jnp.dot(tokens, w_query, preferred_element_type=jnp.float32).astype(jnp.bfloat16)
    keys_proj = jnp.dot(tokens, w_key, preferred_element_type=jnp.float32).astype(jnp.bfloat16)
    values_proj = jnp.dot(tokens, w_value, preferred_element_type=jnp.float32).astype(jnp.bfloat16)
    gate_signal = short_conv(queries.astype(jnp.float32), taps_query).astype(jnp.bfloat16)
    product = (short_conv(keys_proj.astype(jnp.float32), taps_key) * short_conv(values_proj.astype(jnp.float32), taps_value)).astype(jnp.bfloat16)
    length = product.shape[0]
    block_width = 128
    blocks = W // block_width
    signal = product.astype(jnp.float32).reshape(length, blocks, block_width).transpose(1, 0, 2)
    rates = decay_rate.reshape(ORDER, blocks, block_width).transpose(1, 0, 2)
    residues = residue.reshape(ORDER, blocks, block_width).transpose(1, 0, 2)
    skips = skip_gain.reshape(blocks, block_width)
    mixed = lax.map(long_block, (signal, rates, residues, skips))
    mixed_long = mixed.transpose(1, 0, 2).reshape(length, W).astype(jnp.bfloat16)
    gated = (gate_signal.astype(jnp.float32) * mixed_long.astype(jnp.float32)).astype(jnp.bfloat16)
    return jnp.dot(gated, w_out, preferred_element_type=jnp.float32).astype(jnp.bfloat16)
```

```python
import jax
import jax.numpy as jnp
from jax import lax
from jax.sharding import PartitionSpec as P


def short_conv(padded, taps):
    return taps[0] * padded[2:] + taps[1] * padded[1:-1] + taps[2] * padded[:-2]


def modal_long_conv(signal, rates, residues, skips):
    length, width = signal.shape
    order = rates.shape[0]
    ctx_count = lax.axis_size("ctx")
    me = lax.axis_index("ctx")
    coefs = residues * jnp.sqrt(2.0 * rates)
    times = jnp.arange(length, dtype=jnp.float32)[:, None, None]
    grow = jnp.exp(rates[None] * times)
    decay = jnp.exp(-rates[None] * times)
    lifted = (grow * signal[:, None, :]).reshape(length, order * width)
    rows = jnp.arange(length, dtype=jnp.int32)
    lower = (rows[:, None] >= rows[None, :]).astype(jnp.float32)
    running = jnp.matmul(lower, lifted, precision=lax.Precision.HIGHEST).reshape(
        length, order, width
    )
    end_state = running[length - 1] * jnp.exp(-rates * (length - 1))
    states = lax.all_gather(end_state, "ctx", axis=0, tiled=False)
    chunk_ids = jnp.arange(ctx_count, dtype=jnp.int32)
    gap = jnp.maximum(me - 1 - chunk_ids, 0).astype(jnp.float32)
    carry_w = jnp.where(
        (chunk_ids < me)[:, None, None],
        jnp.exp(-rates[None] * (gap[:, None, None] * length)),
        0.0,
    )
    carried = jnp.sum(carry_w * states, axis=0) * jnp.exp(-rates)
    total = running + carried[None]
    mixed = jnp.sum((coefs[None] * decay) * total, axis=1)
    return mixed + skips * signal


def body(
    tokens,
    w_query,
    w_key,
    w_value,
    taps_query,
    taps_key,
    taps_value,
    decay_rate,
    residue,
    skip_gain,
    w_out,
):
    ctx_count = lax.axis_size("ctx")
    halo = lax.ppermute(
        tokens[-2:], "ctx", perm=[(i, i + 1) for i in range(ctx_count - 1)]
    )
    rows = jnp.concatenate([halo, tokens], axis=0)

    def project(piece):
        full = lax.all_gather(piece, "ctx", axis=0, tiled=True)
        out = jnp.dot(rows, full, preferred_element_type=jnp.float32)
        return out.astype(jnp.bfloat16).astype(jnp.float32)

    queries = project(w_query)
    keys_proj = project(w_key)
    values_proj = project(w_value)
    gate = short_conv(queries, taps_query).astype(jnp.bfloat16)
    product = (short_conv(keys_proj, taps_key) * short_conv(values_proj, taps_value)).astype(
        jnp.bfloat16
    )
    mixed = modal_long_conv(product.astype(jnp.float32), decay_rate, residue, skip_gain)
    mixed = mixed.astype(jnp.bfloat16)
    gated = (gate.astype(jnp.float32) * mixed.astype(jnp.float32)).astype(jnp.bfloat16)
    features = lax.all_gather(gated, "tp", axis=1, tiled=True)
    result = jnp.dot(
        features,
        lax.all_gather(w_out, "ctx", axis=0, tiled=True),
        preferred_element_type=jnp.float32,
    )
    return result.astype(jnp.bfloat16)


def solution(mesh):
    in_specs = (
        P("ctx", None),
        P("ctx", "tp"),
        P("ctx", "tp"),
        P("ctx", "tp"),
        P(None, "tp"),
        P(None, "tp"),
        P(None, "tp"),
        P(None, "tp"),
        P(None, "tp"),
        P("tp"),
        P("ctx", "tp"),
    )
    out_specs = P("ctx", "tp")
    return jax.shard_map(body, mesh=mesh, in_specs=in_specs, out_specs=out_specs, check_vma=False)
```

```python
import jax
import jax.numpy as jnp
from jax import lax
from jax.sharding import PartitionSpec as P


def short_conv(padded, taps):
    return taps[0] * padded[2:] + taps[1] * padded[1:-1] + taps[2] * padded[:-2]


def modal_long_conv(signal, rates, residues, skips):
    length, width = signal.shape
    order = rates.shape[0]
    ctx_count = lax.axis_size("ctx")
    me = lax.axis_index("ctx")
    coefs = residues * jnp.sqrt(2.0 * rates)
    times = jnp.arange(length, dtype=jnp.float32)[:, None, None]
    grow = jnp.exp(rates[None] * times)
    decay = jnp.exp(-rates[None] * times)
    lifted = (grow * signal[:, None, :]).reshape(length, order * width)
    rows = jnp.arange(length, dtype=jnp.int32)
    lower = (rows[:, None] >= rows[None, :]).astype(jnp.float32)
    running = jnp.matmul(lower, lifted, precision=lax.Precision.HIGHEST).reshape(
        length, order, width
    )
    end_state = running[length - 1] * jnp.exp(-rates * (length - 1))
    states = lax.all_gather(end_state, "ctx", axis=0, tiled=False)
    chunk_ids = jnp.arange(ctx_count, dtype=jnp.int32)
    gap = jnp.maximum(me - 1 - chunk_ids, 0).astype(jnp.float32)
    carry_w = jnp.where(
        (chunk_ids < me)[:, None, None],
        jnp.exp(-rates[None] * (gap[:, None, None] * length)),
        0.0,
    )
    carried = jnp.sum(carry_w * states, axis=0) * jnp.exp(-rates)
    total = running + carried[None]
    mixed = jnp.sum((coefs[None] * decay) * total, axis=1)
    return mixed + skips * signal


def ring_order(count):
    if count % 2:
        return list(range(count))
    return list(range(0, count, 2)) + list(range(count - 1, 0, -2))


def ring_contract(pieces, consume, acc):
    count = lax.axis_size("ctx")
    ring = ring_order(count)
    place = [0] * count
    for pos, dev in enumerate(ring):
        place[dev] = pos
    fwd = [(ring[k], ring[(k + 1) % count]) for k in range(count)]
    bwd = [(ring[(k + 1) % count], ring[k]) for k in range(count)]
    me = lax.axis_index("ctx")
    my_pos = jnp.array(place, jnp.int32)[me]
    ring_arr = jnp.array(ring, jnp.int32)
    ups = tuple(p[0] for p in pieces)
    lows = tuple(p[1] for p in pieces)
    acc = consume(acc, me, ups, lows, me)
    for step in range(1, count):
        ups = lax.ppermute(ups, "ctx", perm=fwd)
        lows = lax.ppermute(lows, "ctx", perm=bwd)
        src_up = ring_arr[(my_pos - step) % count]
        src_low = ring_arr[(my_pos + step) % count]
        acc = consume(acc, src_up, ups, lows, src_low)
    return acc


def body(
    tokens,
    w_query,
    w_key,
    w_value,
    taps_query,
    taps_key,
    taps_value,
    decay_rate,
    residue,
    skip_gain,
    w_out,
):
    ctx_count = lax.axis_size("ctx")
    halo = lax.ppermute(
        tokens[-2:], "ctx", perm=[(i, i + 1) for i in range(ctx_count - 1)]
    )
    rows = jnp.concatenate([halo, tokens], axis=0)
    d_chunk = w_query.shape[0]
    d_half = d_chunk // 2
    width = w_query.shape[1]
    weights = (w_query, w_key, w_value)
    pieces = [(w[:d_half], w[d_half:]) for w in weights]

    def consume_proj(acc, src_up, ups, lows, src_low):
        cols_up = lax.dynamic_slice_in_dim(rows, src_up * d_chunk, d_half, 1)
        cols_low = lax.dynamic_slice_in_dim(rows, src_low * d_chunk + d_half, d_half, 1)
        return tuple(
            a
            + jnp.dot(cols_up, u, preferred_element_type=jnp.float32)
            + jnp.dot(cols_low, l, preferred_element_type=jnp.float32)
            for a, u, l in zip(acc, ups, lows)
        )

    zero = jnp.zeros((rows.shape[0], width), jnp.float32)
    projected = ring_contract(pieces, consume_proj, (zero, zero, zero))
    queries, keys_proj, values_proj = (
        p.astype(jnp.bfloat16).astype(jnp.float32) for p in projected
    )
    gate = short_conv(queries, taps_query).astype(jnp.bfloat16)
    product = (short_conv(keys_proj, taps_key) * short_conv(values_proj, taps_value)).astype(
        jnp.bfloat16
    )
    mixed = modal_long_conv(product.astype(jnp.float32), decay_rate, residue, skip_gain)
    mixed = mixed.astype(jnp.bfloat16)
    gated = (gate.astype(jnp.float32) * mixed.astype(jnp.float32)).astype(jnp.bfloat16)
    features = lax.all_gather(gated, "tp", axis=1, tiled=True)
    c_chunk = w_out.shape[0]
    c_half = c_chunk // 2

    def consume_out(acc, src_up, ups, lows, src_low):
        cols_up = lax.dynamic_slice_in_dim(features, src_up * c_chunk, c_half, 1)
        cols_low = lax.dynamic_slice_in_dim(features, src_low * c_chunk + c_half, c_half, 1)
        return (
            acc[0]
            + jnp.dot(cols_up, ups[0], preferred_element_type=jnp.float32)
            + jnp.dot(cols_low, lows[0], preferred_element_type=jnp.float32),
        )

    out_zero = jnp.zeros((features.shape[0], w_out.shape[1]), jnp.float32)
    (result,) = ring_contract([(w_out[:c_half], w_out[c_half:])], consume_out, (out_zero,))
    return result.astype(jnp.bfloat16)


def solution(mesh):
    in_specs = (
        P("ctx", None),
        P("ctx", "tp"),
        P("ctx", "tp"),
        P("ctx", "tp"),
        P(None, "tp"),
        P(None, "tp"),
        P(None, "tp"),
        P(None, "tp"),
        P(None, "tp"),
        P("tp"),
        P("ctx", "tp"),
    )
    out_specs = P("ctx", "tp")
    return jax.shard_map(body, mesh=mesh, in_specs=in_specs, out_specs=out_specs, check_vma=False)
```

```python
import jax
import jax.numpy as jnp
from jax import lax
from jax.sharding import PartitionSpec as P


def short_conv(padded, taps):
    return taps[0] * padded[2:] + taps[1] * padded[1:-1] + taps[2] * padded[:-2]


def modal_long_conv(signal, rates, residues, skips):
    length, width = signal.shape
    order = rates.shape[0]
    ctx_count = lax.axis_size("ctx")
    me = lax.axis_index("ctx")
    coefs = residues * jnp.sqrt(2.0 * rates)
    times = jnp.arange(length, dtype=jnp.float32)[:, None, None]
    grow = jnp.exp(rates[None] * times)
    decay = jnp.exp(-rates[None] * times)
    lifted = (grow * signal[:, None, :]).reshape(length, order * width)
    rows = jnp.arange(length, dtype=jnp.int32)
    lower = (rows[:, None] >= rows[None, :]).astype(jnp.float32)
    running = jnp.matmul(lower, lifted, precision=lax.Precision.HIGHEST).reshape(
        length, order, width
    )
    end_state = running[length - 1] * jnp.exp(-rates * (length - 1))
    states = lax.all_gather(end_state[None], "ctx", axis=0, tiled=True)
    chunk_ids = jnp.arange(ctx_count, dtype=jnp.int32)
    gap = jnp.maximum(me - 1 - chunk_ids, 0).astype(jnp.float32)
    carry_w = jnp.where(
        (chunk_ids < me)[:, None, None],
        jnp.exp(-rates[None] * (gap[:, None, None] * length)),
        0.0,
    )
    carried = jnp.sum(carry_w * states, axis=0) * jnp.exp(-rates)
    total = running + carried[None]
    mixed = jnp.sum((coefs[None] * decay) * total, axis=1)
    return mixed + skips * signal


def ring_order(count):
    if count % 2:
        return list(range(count))
    return list(range(0, count, 2)) + list(range(count - 1, 0, -2))


def ring_contract(pieces, consume, acc):
    count = lax.axis_size("ctx")
    ring = ring_order(count)
    place = [0] * count
    for pos, dev in enumerate(ring):
        place[dev] = pos
    fwd = [(ring[k], ring[(k + 1) % count]) for k in range(count)]
    bwd = [(ring[(k + 1) % count], ring[k]) for k in range(count)]
    me = lax.axis_index("ctx")
    my_pos = jnp.array(place, jnp.int32)[me]
    ring_arr = jnp.array(ring, jnp.int32)
    ups = tuple(p[0] for p in pieces)
    lows = tuple(p[1] for p in pieces)
    acc = consume(acc, me, ups, lows, me)
    for step in range(1, count):
        ups = lax.ppermute(ups, "ctx", perm=fwd)
        lows = lax.ppermute(lows, "ctx", perm=bwd)
        src_up = ring_arr[(my_pos - step) % count]
        src_low = ring_arr[(my_pos + step) % count]
        acc = consume(acc, src_up, ups, lows, src_low)
    return acc


def ring_reduce_scatter(piece, count):
    ring = ring_order(count)
    place = [0] * count
    for pos, dev in enumerate(ring):
        place[dev] = pos
    fwd = [(ring[k], ring[(k + 1) % count]) for k in range(count)]
    bwd = [(ring[(k + 1) % count], ring[k]) for k in range(count)]
    me = lax.axis_index("ctx")
    my_pos = jnp.array(place, jnp.int32)[me]
    ring_arr = jnp.array(ring, jnp.int32)
    up = piece(ring_arr[(my_pos - 1) % count], 0)
    down = piece(ring_arr[(my_pos + 1) % count], 1)
    for step in range(1, count):
        up = lax.ppermute(up.astype(jnp.bfloat16), "ctx", perm=fwd).astype(jnp.float32)
        down = lax.ppermute(down.astype(jnp.bfloat16), "ctx", perm=bwd).astype(jnp.float32)
        up = up + piece(ring_arr[(my_pos - step - 1) % count], 0)
        down = down + piece(ring_arr[(my_pos + step + 1) % count], 1)
    return up, down


def body(
    tokens,
    w_query,
    w_key,
    w_value,
    taps_query,
    taps_key,
    taps_value,
    decay_rate,
    residue,
    skip_gain,
    w_out,
):
    ctx_count = lax.axis_size("ctx")
    length = tokens.shape[0]
    width = w_query.shape[1]
    columns = lax.all_to_all(tokens, "ctx", split_axis=1, concat_axis=0, tiled=True)
    columns = jnp.concatenate([jnp.zeros((2, columns.shape[1]), columns.dtype), columns], axis=0)
    w_cat = jnp.concatenate([w_query, w_key, w_value], axis=1)
    split = w_cat.shape[1] // 2
    halves = (w_cat[:, :split], w_cat[:, split:])

    def piece(dest, side):
        rows = lax.dynamic_slice_in_dim(columns, dest * length, length + 2, 0)
        return jnp.dot(rows, halves[side], preferred_element_type=jnp.float32)

    up, down = ring_reduce_scatter(piece, ctx_count)
    projected = jnp.concatenate([up, down], axis=1).astype(jnp.bfloat16).astype(jnp.float32)
    queries = projected[:, :width]
    keys_proj = projected[:, width : 2 * width]
    values_proj = projected[:, 2 * width :]
    gate = short_conv(queries, taps_query).astype(jnp.bfloat16)
    product = (short_conv(keys_proj, taps_key) * short_conv(values_proj, taps_value)).astype(
        jnp.bfloat16
    )
    mixed = modal_long_conv(product.astype(jnp.float32), decay_rate, residue, skip_gain)
    mixed = mixed.astype(jnp.bfloat16)
    gated = (gate.astype(jnp.float32) * mixed.astype(jnp.float32)).astype(jnp.bfloat16)
    features = lax.all_gather(gated, "tp", axis=1, tiled=True)
    c_chunk = w_out.shape[0]
    c_half = c_chunk // 2

    def consume_out(acc, src_up, ups, lows, src_low):
        cols_up = lax.dynamic_slice_in_dim(features, src_up * c_chunk, c_half, 1)
        cols_low = lax.dynamic_slice_in_dim(features, src_low * c_chunk + c_half, c_half, 1)
        return (
            acc[0]
            + jnp.dot(cols_up, ups[0], preferred_element_type=jnp.float32)
            + jnp.dot(cols_low, lows[0], preferred_element_type=jnp.float32),
        )

    out_zero = jnp.zeros((features.shape[0], w_out.shape[1]), jnp.float32)
    (result,) = ring_contract([(w_out[:c_half], w_out[c_half:])], consume_out, (out_zero,))
    return result.astype(jnp.bfloat16)


def solution(mesh):
    in_specs = (
        P("ctx", None),
        P("ctx", "tp"),
        P("ctx", "tp"),
        P("ctx", "tp"),
        P(None, "tp"),
        P(None, "tp"),
        P(None, "tp"),
        P(None, "tp"),
        P(None, "tp"),
        P("tp"),
        P("ctx", "tp"),
    )
    out_specs = P("ctx", "tp")
    return jax.shard_map(body, mesh=mesh, in_specs=in_specs, out_specs=out_specs, check_vma=False)
```

```python
import jax
import jax.numpy as jnp
from jax import lax
from jax.sharding import PartitionSpec as P


def short_conv(padded, taps):
    return taps[0] * padded[2:] + taps[1] * padded[1:-1] + taps[2] * padded[:-2]


def modal_long_conv(signal, rates, residues, skips):
    length, width = signal.shape
    order = rates.shape[0]
    ctx_count = lax.axis_size("ctx")
    coefs = residues * jnp.sqrt(2.0 * rates)
    times = jnp.arange(length, dtype=jnp.float32)[:, None, None]
    grow = jnp.exp(rates[None] * times)
    decay = jnp.exp(-rates[None] * times)
    lifted = (grow * signal[:, None, :]).reshape(length, order * width)
    rows = jnp.arange(length, dtype=jnp.int32)
    lower = (rows[:, None] >= rows[None, :]).astype(jnp.float32)
    running = jnp.matmul(lower, lifted, precision=lax.Precision.HIGHEST).reshape(
        length, order, width
    )
    end_state = running[length - 1] * jnp.exp(-rates * (length - 1))
    carried = jnp.zeros_like(end_state)
    for shift in range(1, ctx_count):
        earlier = lax.ppermute(
            end_state, "ctx", perm=[(i, i + shift) for i in range(ctx_count - shift)]
        )
        carried = carried + jnp.exp(-rates * (length * (shift - 1))) * earlier
    carried = carried * jnp.exp(-rates)
    total = running + carried[None]
    mixed = jnp.sum((coefs[None] * decay) * total, axis=1)
    return mixed + skips * signal


def ring_order(count):
    if count % 2:
        return list(range(count))
    return list(range(0, count, 2)) + list(range(count - 1, 0, -2))


def ring_contract(pieces, consume, acc):
    count = lax.axis_size("ctx")
    ring = ring_order(count)
    place = [0] * count
    for pos, dev in enumerate(ring):
        place[dev] = pos
    fwd = [(ring[k], ring[(k + 1) % count]) for k in range(count)]
    bwd = [(ring[(k + 1) % count], ring[k]) for k in range(count)]
    me = lax.axis_index("ctx")
    my_pos = jnp.array(place, jnp.int32)[me]
    ring_arr = jnp.array(ring, jnp.int32)
    ups = tuple(p[0] for p in pieces)
    lows = tuple(p[1] for p in pieces)
    acc = consume(acc, me, ups, lows, me)
    for step in range(1, count):
        ups = lax.ppermute(ups, "ctx", perm=fwd)
        lows = lax.ppermute(lows, "ctx", perm=bwd)
        src_up = ring_arr[(my_pos - step) % count]
        src_low = ring_arr[(my_pos + step) % count]
        acc = consume(acc, src_up, ups, lows, src_low)
    return acc


def ring_reduce_scatter(piece, count):
    ring = ring_order(count)
    place = [0] * count
    for pos, dev in enumerate(ring):
        place[dev] = pos
    fwd = [(ring[k], ring[(k + 1) % count]) for k in range(count)]
    bwd = [(ring[(k + 1) % count], ring[k]) for k in range(count)]
    me = lax.axis_index("ctx")
    my_pos = jnp.array(place, jnp.int32)[me]
    ring_arr = jnp.array(ring, jnp.int32)
    up = piece(ring_arr[(my_pos - 1) % count], 0)
    down = piece(ring_arr[(my_pos + 1) % count], 1)
    for step in range(1, count):
        up = lax.ppermute(up.astype(jnp.bfloat16), "ctx", perm=fwd).astype(jnp.float32)
        down = lax.ppermute(down.astype(jnp.bfloat16), "ctx", perm=bwd).astype(jnp.float32)
        up = up + piece(ring_arr[(my_pos - step - 1) % count], 0)
        down = down + piece(ring_arr[(my_pos + step + 1) % count], 1)
    return up, down


def body(
    tokens,
    w_query,
    w_key,
    w_value,
    taps_query,
    taps_key,
    taps_value,
    decay_rate,
    residue,
    skip_gain,
    w_out,
):
    ctx_count = lax.axis_size("ctx")
    length = tokens.shape[0]
    width = w_query.shape[1]
    columns = lax.all_to_all(tokens, "ctx", split_axis=1, concat_axis=0, tiled=True)
    columns = jnp.concatenate([jnp.zeros((2, columns.shape[1]), columns.dtype), columns], axis=0)
    w_cat = jnp.concatenate([w_query, w_key, w_value], axis=1)
    split = w_cat.shape[1] // 2
    halves = (w_cat[:, :split], w_cat[:, split:])

    def piece(dest, side):
        rows = lax.dynamic_slice_in_dim(columns, dest * length, length + 2, 0)
        return jnp.dot(rows, halves[side], preferred_element_type=jnp.float32)

    up, down = ring_reduce_scatter(piece, ctx_count)
    projected = jnp.concatenate([up, down], axis=1).astype(jnp.bfloat16).astype(jnp.float32)
    queries = projected[:, :width]
    keys_proj = projected[:, width : 2 * width]
    values_proj = projected[:, 2 * width :]
    gate = short_conv(queries, taps_query).astype(jnp.bfloat16)
    product = (short_conv(keys_proj, taps_key) * short_conv(values_proj, taps_value)).astype(
        jnp.bfloat16
    )
    mixed = modal_long_conv(product.astype(jnp.float32), decay_rate, residue, skip_gain)
    mixed = mixed.astype(jnp.bfloat16)
    gated = (gate.astype(jnp.float32) * mixed.astype(jnp.float32)).astype(jnp.bfloat16)
    features = lax.all_gather(gated, "tp", axis=1, tiled=True)
    c_chunk = w_out.shape[0]
    c_half = c_chunk // 2

    def place_out(acc, src_up, ups, lows, src_low):
        acc = lax.dynamic_update_slice_in_dim(acc, ups[0][None], src_up * 2, 0)
        return lax.dynamic_update_slice_in_dim(acc, lows[0][None], src_low * 2 + 1, 0)

    blank = jnp.zeros((2 * ctx_count, c_half, w_out.shape[1]), w_out.dtype)
    w_full = ring_contract([(w_out[:c_half], w_out[c_half:])], place_out, blank)
    w_full = w_full.reshape(ctx_count * c_chunk, w_out.shape[1])
    result = jnp.dot(features, w_full, preferred_element_type=jnp.float32)
    return result.astype(jnp.bfloat16)


def solution(mesh):
    in_specs = (
        P("ctx", None),
        P("ctx", "tp"),
        P("ctx", "tp"),
        P("ctx", "tp"),
        P(None, "tp"),
        P(None, "tp"),
        P(None, "tp"),
        P(None, "tp"),
        P(None, "tp"),
        P("tp"),
        P("ctx", "tp"),
    )
    out_specs = P("ctx", "tp")
    return jax.shard_map(body, mesh=mesh, in_specs=in_specs, out_specs=out_specs, check_vma=False)
```

```python
import jax
import jax.numpy as jnp
from jax import lax
from jax.sharding import PartitionSpec as P


def short_conv(padded, taps):
    return taps[0] * padded[2:] + taps[1] * padded[1:-1] + taps[2] * padded[:-2]


def modal_long_conv(signal, rates, residues, skips):
    length, width = signal.shape
    order = rates.shape[0]
    ctx_count = lax.axis_size("ctx")
    coefs = residues * jnp.sqrt(2.0 * rates)
    times = jnp.arange(length, dtype=jnp.float32)[:, None, None]
    grow = jnp.exp(rates[None] * times)
    decay = jnp.exp(-rates[None] * times)
    lifted = (grow * signal[:, None, :]).reshape(length, order * width)
    rows = jnp.arange(length, dtype=jnp.int32)
    lower = (rows[:, None] >= rows[None, :]).astype(jnp.float32)
    running = jnp.matmul(lower, lifted, precision=lax.Precision.HIGHEST).reshape(
        length, order, width
    )
    end_state = running[length - 1] * jnp.exp(-rates * (length - 1))
    carried = jnp.zeros_like(end_state)
    for shift in range(1, ctx_count):
        earlier = lax.ppermute(
            end_state, "ctx", perm=[(i, i + shift) for i in range(ctx_count - shift)]
        )
        carried = carried + jnp.exp(-rates * (length * (shift - 1))) * earlier
    carried = carried * jnp.exp(-rates)
    total = running + carried[None]
    mixed = jnp.sum((coefs[None] * decay) * total, axis=1)
    return mixed + skips * signal


def ring_order(count):
    if count % 2:
        return list(range(count))
    return list(range(0, count, 2)) + list(range(count - 1, 0, -2))


def body(
    tokens,
    w_query,
    w_key,
    w_value,
    taps_query,
    taps_key,
    taps_value,
    decay_rate,
    residue,
    skip_gain,
    w_out,
):
    ctx_count = lax.axis_size("ctx")
    length = tokens.shape[0]
    width = w_query.shape[1]
    columns = lax.all_to_all(tokens, "ctx", split_axis=1, concat_axis=0, tiled=True)
    columns = jnp.concatenate([jnp.zeros((2, columns.shape[1]), columns.dtype), columns], axis=0)
    w_cat = jnp.concatenate([w_query, w_key, w_value], axis=1)
    split = w_cat.shape[1] // 2
    halves = (w_cat[:, :split], w_cat[:, split:])

    def piece(dest, side):
        rows = lax.dynamic_slice_in_dim(columns, dest * length, length + 2, 0)
        return jnp.dot(rows, halves[side], preferred_element_type=jnp.float32)

    ring = ring_order(ctx_count)
    place = [0] * ctx_count
    for pos, dev in enumerate(ring):
        place[dev] = pos
    fwd = [(ring[k], ring[(k + 1) % ctx_count]) for k in range(ctx_count)]
    bwd = [(ring[(k + 1) % ctx_count], ring[k]) for k in range(ctx_count)]
    me = lax.axis_index("ctx")
    my_pos = jnp.array(place, jnp.int32)[me]
    ring_arr = jnp.array(ring, jnp.int32)
    c_chunk = w_out.shape[0]
    c_half = c_chunk // 2
    w_up, w_low, columns = lax.optimization_barrier((w_out[:c_half], w_out[c_half:], columns))
    w_rows = jnp.zeros((2 * ctx_count, c_half, w_out.shape[1]), w_out.dtype)
    w_rows = lax.dynamic_update_slice_in_dim(w_rows, w_up[None], me * 2, 0)
    w_rows = lax.dynamic_update_slice_in_dim(w_rows, w_low[None], me * 2 + 1, 0)
    up = piece(ring_arr[(my_pos - 1) % ctx_count], 0)
    down = piece(ring_arr[(my_pos + 1) % ctx_count], 1)
    for step in range(1, ctx_count):
        sent = lax.optimization_barrier(
            (up.astype(jnp.bfloat16), down.astype(jnp.bfloat16), w_up, w_low)
        )
        up, w_up = lax.ppermute((sent[0], sent[2]), "ctx", perm=fwd)
        down, w_low = lax.ppermute((sent[1], sent[3]), "ctx", perm=bwd)
        src_up = ring_arr[(my_pos - step) % ctx_count]
        src_low = ring_arr[(my_pos + step) % ctx_count]
        w_rows = lax.dynamic_update_slice_in_dim(w_rows, w_up[None], src_up * 2, 0)
        w_rows = lax.dynamic_update_slice_in_dim(w_rows, w_low[None], src_low * 2 + 1, 0)
        up = up.astype(jnp.float32) + piece(ring_arr[(my_pos - step - 1) % ctx_count], 0)
        down = down.astype(jnp.float32) + piece(ring_arr[(my_pos + step + 1) % ctx_count], 1)

    projected = jnp.concatenate([up, down], axis=1).astype(jnp.bfloat16).astype(jnp.float32)
    queries = projected[:, :width]
    keys_proj = projected[:, width : 2 * width]
    values_proj = projected[:, 2 * width :]
    gate = short_conv(queries, taps_query).astype(jnp.bfloat16)
    product = (short_conv(keys_proj, taps_key) * short_conv(values_proj, taps_value)).astype(
        jnp.bfloat16
    )
    mixed = modal_long_conv(product.astype(jnp.float32), decay_rate, residue, skip_gain)
    mixed = mixed.astype(jnp.bfloat16)
    gated = (gate.astype(jnp.float32) * mixed.astype(jnp.float32)).astype(jnp.bfloat16)
    features = lax.all_gather(gated, "tp", axis=1, tiled=True)
    w_full = w_rows.reshape(ctx_count * c_chunk, w_out.shape[1])
    result = jnp.dot(features, w_full, preferred_element_type=jnp.float32)
    return result.astype(jnp.bfloat16)


def solution(mesh):
    in_specs = (
        P("ctx", None),
        P("ctx", "tp"),
        P("ctx", "tp"),
        P("ctx", "tp"),
        P(None, "tp"),
        P(None, "tp"),
        P(None, "tp"),
        P(None, "tp"),
        P(None, "tp"),
        P("tp"),
        P("ctx", "tp"),
    )
    out_specs = P("ctx", "tp")
    return jax.shard_map(body, mesh=mesh, in_specs=in_specs, out_specs=out_specs, check_vma=False)
```

```python
import jax
import jax.numpy as jnp
from jax import lax
from jax.sharding import PartitionSpec as P


def short_conv(padded, taps):
    return taps[0] * padded[2:] + taps[1] * padded[1:-1] + taps[2] * padded[:-2]


def modal_long_conv(signal, rates, residues, skips):
    length, width = signal.shape
    order = rates.shape[0]
    ctx_count = lax.axis_size("ctx")
    coefs = residues * jnp.sqrt(2.0 * rates)
    times = jnp.arange(length, dtype=jnp.float32)[None, :, None]
    grow = jnp.exp(rates[:, None, :] * times)
    decay = jnp.exp(-rates[:, None, :] * times)
    lifted = grow * signal[None]
    rows = jnp.arange(length, dtype=jnp.int32)
    lower = (rows[:, None] >= rows[None, :]).astype(jnp.float32)
    lower = jnp.broadcast_to(lower[None], (order, length, length))
    running = lax.dot_general(
        lower,
        lifted,
        (((2,), (1,)), ((0,), (0,))),
        precision=lax.Precision.HIGHEST,
        preferred_element_type=jnp.float32,
    )
    end_state = running[:, length - 1] * jnp.exp(-rates * (length - 1))
    carried = jnp.zeros_like(end_state)
    for shift in range(1, ctx_count):
        earlier = lax.ppermute(
            end_state, "ctx", perm=[(i, i + shift) for i in range(ctx_count - shift)]
        )
        carried = carried + jnp.exp(-rates * (length * (shift - 1))) * earlier
    carried = carried * jnp.exp(-rates)
    total = running + carried[:, None, :]
    mixed = jnp.sum((coefs[:, None, :] * decay) * total, axis=0)
    return mixed + skips * signal


def ring_order(count):
    if count % 2:
        return list(range(count))
    return list(range(0, count, 2)) + list(range(count - 1, 0, -2))


def body(
    tokens,
    w_query,
    w_key,
    w_value,
    taps_query,
    taps_key,
    taps_value,
    decay_rate,
    residue,
    skip_gain,
    w_out,
):
    ctx_count = lax.axis_size("ctx")
    length = tokens.shape[0]
    width = w_query.shape[1]
    columns = lax.all_to_all(tokens, "ctx", split_axis=1, concat_axis=0, tiled=True)
    columns = jnp.concatenate([jnp.zeros((2, columns.shape[1]), columns.dtype), columns], axis=0)
    w_cat = jnp.concatenate([w_query, w_key, w_value], axis=1)
    split = w_cat.shape[1] // 2
    halves = (w_cat[:, :split], w_cat[:, split:])

    def piece(dest, side):
        rows = lax.dynamic_slice_in_dim(columns, dest * length, length + 2, 0)
        return jnp.dot(rows, halves[side], preferred_element_type=jnp.float32)

    ring = ring_order(ctx_count)
    place = [0] * ctx_count
    for pos, dev in enumerate(ring):
        place[dev] = pos
    fwd = [(ring[k], ring[(k + 1) % ctx_count]) for k in range(ctx_count)]
    bwd = [(ring[(k + 1) % ctx_count], ring[k]) for k in range(ctx_count)]
    me = lax.axis_index("ctx")
    my_pos = jnp.array(place, jnp.int32)[me]
    ring_arr = jnp.array(ring, jnp.int32)
    c_chunk = w_out.shape[0]
    c_half = c_chunk // 2
    up = piece(ring_arr[(my_pos - 1) % ctx_count], 0)
    down = piece(ring_arr[(my_pos + 1) % ctx_count], 1)
    for step in range(1, ctx_count):
        up = lax.ppermute(up.astype(jnp.bfloat16), "ctx", perm=fwd).astype(jnp.float32)
        down = lax.ppermute(down.astype(jnp.bfloat16), "ctx", perm=bwd).astype(jnp.float32)
        up = up + piece(ring_arr[(my_pos - step - 1) % ctx_count], 0)
        down = down + piece(ring_arr[(my_pos + step + 1) % ctx_count], 1)
    w_up, w_low, up, down = lax.optimization_barrier(
        (w_out[:c_half], w_out[c_half:], up, down)
    )
    w_rows = jnp.zeros((2 * ctx_count, c_half, w_out.shape[1]), w_out.dtype)
    w_rows = lax.dynamic_update_slice_in_dim(w_rows, w_up[None], me * 2, 0)
    w_rows = lax.dynamic_update_slice_in_dim(w_rows, w_low[None], me * 2 + 1, 0)
    for step in range(1, ctx_count):
        w_up = lax.ppermute(w_up, "ctx", perm=fwd)
        w_low = lax.ppermute(w_low, "ctx", perm=bwd)
        src_up = ring_arr[(my_pos - step) % ctx_count]
        src_low = ring_arr[(my_pos + step) % ctx_count]
        w_rows = lax.dynamic_update_slice_in_dim(w_rows, w_up[None], src_up * 2, 0)
        w_rows = lax.dynamic_update_slice_in_dim(w_rows, w_low[None], src_low * 2 + 1, 0)

    projected = jnp.concatenate([up, down], axis=1).astype(jnp.bfloat16).astype(jnp.float32)
    queries = projected[:, :width]
    keys_proj = projected[:, width : 2 * width]
    values_proj = projected[:, 2 * width :]
    gate = short_conv(queries, taps_query).astype(jnp.bfloat16)
    product = (short_conv(keys_proj, taps_key) * short_conv(values_proj, taps_value)).astype(
        jnp.bfloat16
    )
    mixed = modal_long_conv(product.astype(jnp.float32), decay_rate, residue, skip_gain)
    mixed = mixed.astype(jnp.bfloat16)
    gated = (gate.astype(jnp.float32) * mixed.astype(jnp.float32)).astype(jnp.bfloat16)
    features = lax.all_gather(gated, "tp", axis=1, tiled=True)
    w_full = w_rows.reshape(ctx_count * c_chunk, w_out.shape[1])
    result = jnp.dot(features, w_full, preferred_element_type=jnp.float32)
    return result.astype(jnp.bfloat16)


def solution(mesh):
    in_specs = (
        P("ctx", None),
        P("ctx", "tp"),
        P("ctx", "tp"),
        P("ctx", "tp"),
        P(None, "tp"),
        P(None, "tp"),
        P(None, "tp"),
        P(None, "tp"),
        P(None, "tp"),
        P("tp"),
        P("ctx", "tp"),
    )
    out_specs = P("ctx", "tp")
    return jax.shard_map(body, mesh=mesh, in_specs=in_specs, out_specs=out_specs, check_vma=False)
```

```python
import jax
import jax.numpy as jnp
from jax import lax
from jax.sharding import PartitionSpec as P


def short_conv(padded, taps):
    return taps[0] * padded[2:] + taps[1] * padded[1:-1] + taps[2] * padded[:-2]


def modal_long_conv(signal, rates, residues, skips):
    length, width = signal.shape
    order = rates.shape[0]
    ctx_count = lax.axis_size("ctx")
    coefs = residues * jnp.sqrt(2.0 * rates)
    times = jnp.arange(length, dtype=jnp.float32)[None, :, None]
    grow = jnp.exp(rates[:, None, :] * times)
    decay = jnp.exp(-rates[:, None, :] * times)
    lifted = grow * signal[None]
    rows = jnp.arange(length, dtype=jnp.int32)
    lower = (rows[:, None] >= rows[None, :]).astype(jnp.float32)
    lower = jnp.broadcast_to(lower[None], (order, length, length))
    running = lax.dot_general(
        lower,
        lifted,
        (((2,), (1,)), ((0,), (0,))),
        precision=lax.Precision.HIGHEST,
        preferred_element_type=jnp.float32,
    )
    end_state = running[:, length - 1] * jnp.exp(-rates * (length - 1))
    carried = jnp.zeros_like(end_state)
    for shift in range(1, ctx_count):
        earlier = lax.ppermute(
            end_state, "ctx", perm=[(i, i + shift) for i in range(ctx_count - shift)]
        )
        carried = carried + jnp.exp(-rates * (length * (shift - 1))) * earlier
    carried = carried * jnp.exp(-rates)
    total = running + carried[:, None, :]
    mixed = jnp.sum((coefs[:, None, :] * decay) * total, axis=0)
    return mixed + skips * signal


def ring_order(count):
    if count % 2:
        return list(range(count))
    return list(range(0, count, 2)) + list(range(count - 1, 0, -2))


def body(
    tokens,
    w_query,
    w_key,
    w_value,
    taps_query,
    taps_key,
    taps_value,
    decay_rate,
    residue,
    skip_gain,
    w_out,
):
    ctx_count = lax.axis_size("ctx")
    length = tokens.shape[0]
    width = w_query.shape[1]
    tp_count = lax.axis_size("tp")
    if tp_count % 2 == 0 and length % 2 == 0:
        half = length // 2
        core = lax.axis_index("tp") % 2
        mine = lax.dynamic_slice_in_dim(tokens, core * half, half, 0)
        mine = lax.all_to_all(mine, "ctx", split_axis=1, concat_axis=0, tiled=True)
        pairs = [(k, k ^ 1) for k in range(tp_count)]
        other = lax.ppermute(mine, "tp", perm=pairs)
        first = jnp.where(core == 0, mine, other).reshape(ctx_count, half, -1)
        second = jnp.where(core == 0, other, mine).reshape(ctx_count, half, -1)
        columns = jnp.concatenate([first, second], axis=1).reshape(ctx_count * length, -1)
    else:
        columns = lax.all_to_all(tokens, "ctx", split_axis=1, concat_axis=0, tiled=True)
    columns = jnp.concatenate([jnp.zeros((2, columns.shape[1]), columns.dtype), columns], axis=0)
    w_cat = jnp.concatenate([w_query, w_key, w_value], axis=1)
    split = w_cat.shape[1] // 2
    halves = (w_cat[:, :split], w_cat[:, split:])

    def piece(dest, side):
        rows = lax.dynamic_slice_in_dim(columns, dest * length, length + 2, 0)
        return jnp.dot(rows, halves[side], preferred_element_type=jnp.float32)

    ring = ring_order(ctx_count)
    place = [0] * ctx_count
    for pos, dev in enumerate(ring):
        place[dev] = pos
    fwd = [(ring[k], ring[(k + 1) % ctx_count]) for k in range(ctx_count)]
    bwd = [(ring[(k + 1) % ctx_count], ring[k]) for k in range(ctx_count)]
    me = lax.axis_index("ctx")
    my_pos = jnp.array(place, jnp.int32)[me]
    ring_arr = jnp.array(ring, jnp.int32)
    c_chunk = w_out.shape[0]
    c_half = c_chunk // 2
    w_up, w_low, columns = lax.optimization_barrier((w_out[:c_half], w_out[c_half:], columns))
    w_rows = jnp.zeros((2 * ctx_count, c_half, w_out.shape[1]), w_out.dtype)
    w_rows = lax.dynamic_update_slice_in_dim(w_rows, w_up[None], me * 2, 0)
    w_rows = lax.dynamic_update_slice_in_dim(w_rows, w_low[None], me * 2 + 1, 0)
    up = piece(ring_arr[(my_pos - 1) % ctx_count], 0)
    down = piece(ring_arr[(my_pos + 1) % ctx_count], 1)
    for step in range(1, ctx_count):
        sent = lax.optimization_barrier(
            (up.astype(jnp.bfloat16), down.astype(jnp.bfloat16), w_up, w_low)
        )
        up, w_up = lax.ppermute((sent[0], sent[2]), "ctx", perm=fwd)
        down, w_low = lax.ppermute((sent[1], sent[3]), "ctx", perm=bwd)
        src_up = ring_arr[(my_pos - step) % ctx_count]
        src_low = ring_arr[(my_pos + step) % ctx_count]
        w_rows = lax.dynamic_update_slice_in_dim(w_rows, w_up[None], src_up * 2, 0)
        w_rows = lax.dynamic_update_slice_in_dim(w_rows, w_low[None], src_low * 2 + 1, 0)
        up = up.astype(jnp.float32) + piece(ring_arr[(my_pos - step - 1) % ctx_count], 0)
        down = down.astype(jnp.float32) + piece(ring_arr[(my_pos + step + 1) % ctx_count], 1)

    projected = jnp.concatenate([up, down], axis=1).astype(jnp.bfloat16).astype(jnp.float32)
    queries = projected[:, :width]
    keys_proj = projected[:, width : 2 * width]
    values_proj = projected[:, 2 * width :]
    gate = short_conv(queries, taps_query).astype(jnp.bfloat16)
    product = (short_conv(keys_proj, taps_key) * short_conv(values_proj, taps_value)).astype(
        jnp.bfloat16
    )
    mixed = modal_long_conv(product.astype(jnp.float32), decay_rate, residue, skip_gain)
    mixed = mixed.astype(jnp.bfloat16)
    gated = (gate.astype(jnp.float32) * mixed.astype(jnp.float32)).astype(jnp.bfloat16)
    features = lax.all_gather(gated, "tp", axis=1, tiled=True)
    w_full = w_rows.reshape(ctx_count * c_chunk, w_out.shape[1])
    result = jnp.dot(features, w_full, preferred_element_type=jnp.float32)
    return result.astype(jnp.bfloat16)


def solution(mesh):
    in_specs = (
        P("ctx", None),
        P("ctx", "tp"),
        P("ctx", "tp"),
        P("ctx", "tp"),
        P(None, "tp"),
        P(None, "tp"),
        P(None, "tp"),
        P(None, "tp"),
        P(None, "tp"),
        P("tp"),
        P("ctx", "tp"),
    )
    out_specs = P("ctx", "tp")
    return jax.shard_map(body, mesh=mesh, in_specs=in_specs, out_specs=out_specs, check_vma=False)
```

```python
import jax
import jax.numpy as jnp
from jax import lax
from jax.sharding import PartitionSpec as P


def short_conv(padded, taps):
    return taps[0] * padded[2:] + taps[1] * padded[1:-1] + taps[2] * padded[:-2]


def modal_long_conv(signal, rates, residues, skips):
    length, width = signal.shape
    order = rates.shape[0]
    ctx_count = lax.axis_size("ctx")
    coefs = residues * jnp.sqrt(2.0 * rates)
    times = jnp.arange(length, dtype=jnp.float32)[None, :, None]
    grow = jnp.exp(rates[:, None, :] * times)
    decay = jnp.exp(-rates[:, None, :] * times)
    lifted = grow * signal[None]
    rows = jnp.arange(length, dtype=jnp.int32)
    lower = (rows[:, None] >= rows[None, :]).astype(jnp.float32)
    lower = jnp.broadcast_to(lower[None], (order, length, length))
    running = lax.dot_general(
        lower,
        lifted,
        (((2,), (1,)), ((0,), (0,))),
        precision=lax.Precision.HIGHEST,
        preferred_element_type=jnp.float32,
    )
    end_state = running[:, length - 1] * jnp.exp(-rates * (length - 1))
    carried = jnp.zeros_like(end_state)
    for shift in range(1, ctx_count):
        earlier = lax.ppermute(
            end_state, "ctx", perm=[(i, i + shift) for i in range(ctx_count - shift)]
        )
        carried = carried + jnp.exp(-rates * (length * (shift - 1))) * earlier
    carried = carried * jnp.exp(-rates)
    total = running + carried[:, None, :]
    mixed = jnp.sum((coefs[:, None, :] * decay) * total, axis=0)
    return mixed + skips * signal


def ring_order(count):
    if count % 2:
        return list(range(count))
    return list(range(0, count, 2)) + list(range(count - 1, 0, -2))


def body(
    tokens,
    w_query,
    w_key,
    w_value,
    taps_query,
    taps_key,
    taps_value,
    decay_rate,
    residue,
    skip_gain,
    w_out,
):
    ctx_count = lax.axis_size("ctx")
    length = tokens.shape[0]
    width = w_query.shape[1]
    columns = lax.all_to_all(tokens, "ctx", split_axis=1, concat_axis=0, tiled=True)
    columns = jnp.concatenate([jnp.zeros((2, columns.shape[1]), columns.dtype), columns], axis=0)
    w_cat = jnp.concatenate([w_query, w_key, w_value], axis=1)
    split = w_cat.shape[1] // 2
    halves = (w_cat[:, :split], w_cat[:, split:])

    def piece(dest, side):
        rows = lax.dynamic_slice_in_dim(columns, dest * length, length + 2, 0)
        return jnp.dot(rows, halves[side], preferred_element_type=jnp.float32)

    ring = ring_order(ctx_count)
    place = [0] * ctx_count
    for pos, dev in enumerate(ring):
        place[dev] = pos
    fwd = [(ring[k], ring[(k + 1) % ctx_count]) for k in range(ctx_count)]
    bwd = [(ring[(k + 1) % ctx_count], ring[k]) for k in range(ctx_count)]
    me = lax.axis_index("ctx")
    my_pos = jnp.array(place, jnp.int32)[me]
    ring_arr = jnp.array(ring, jnp.int32)
    c_chunk = w_out.shape[0]
    c_half = c_chunk // 2
    w_up, w_low, columns = lax.optimization_barrier((w_out[:c_half], w_out[c_half:], columns))
    w_rows = jnp.zeros((2 * ctx_count, c_half, w_out.shape[1]), w_out.dtype)
    w_rows = lax.dynamic_update_slice_in_dim(w_rows, w_up[None], me * 2, 0)
    w_rows = lax.dynamic_update_slice_in_dim(w_rows, w_low[None], me * 2 + 1, 0)
    up = piece(ring_arr[(my_pos - 1) % ctx_count], 0)
    down = piece(ring_arr[(my_pos + 1) % ctx_count], 1)
    for step in range(1, ctx_count):
        sent = lax.optimization_barrier(
            (up.astype(jnp.bfloat16), down.astype(jnp.bfloat16), w_up, w_low)
        )
        up, w_up = lax.ppermute((sent[0], sent[2]), "ctx", perm=fwd)
        down, w_low = lax.ppermute((sent[1], sent[3]), "ctx", perm=bwd)
        src_up = ring_arr[(my_pos - step) % ctx_count]
        src_low = ring_arr[(my_pos + step) % ctx_count]
        w_rows = lax.dynamic_update_slice_in_dim(w_rows, w_up[None], src_up * 2, 0)
        w_rows = lax.dynamic_update_slice_in_dim(w_rows, w_low[None], src_low * 2 + 1, 0)
        up = up.astype(jnp.float32) + piece(ring_arr[(my_pos - step - 1) % ctx_count], 0)
        down = down.astype(jnp.float32) + piece(ring_arr[(my_pos + step + 1) % ctx_count], 1)

    projected = jnp.concatenate([up, down], axis=1).astype(jnp.bfloat16).astype(jnp.float32)
    queries = projected[:, :width]
    keys_proj = projected[:, width : 2 * width]
    values_proj = projected[:, 2 * width :]
    gate = short_conv(queries, taps_query).astype(jnp.bfloat16)
    product = (short_conv(keys_proj, taps_key) * short_conv(values_proj, taps_value)).astype(
        jnp.bfloat16
    )
    mixed = modal_long_conv(product.astype(jnp.float32), decay_rate, residue, skip_gain)
    mixed = mixed.astype(jnp.bfloat16)
    gated = (gate.astype(jnp.float32) * mixed.astype(jnp.float32)).astype(jnp.bfloat16)
    features = lax.all_gather(gated, "tp", axis=1, tiled=True)
    w_full = w_rows.reshape(ctx_count * c_chunk, w_out.shape[1])
    result = jnp.dot(features, w_full, preferred_element_type=jnp.float32)
    return result.astype(jnp.bfloat16)


def solution(mesh):
    in_specs = (
        P("ctx", None),
        P("ctx", "tp"),
        P("ctx", "tp"),
        P("ctx", "tp"),
        P(None, "tp"),
        P(None, "tp"),
        P(None, "tp"),
        P(None, "tp"),
        P(None, "tp"),
        P("tp"),
        P("ctx", "tp"),
    )
    out_specs = P("ctx", "tp")
    return jax.shard_map(body, mesh=mesh, in_specs=in_specs, out_specs=out_specs, check_vma=False)
```

```python
import jax
import jax.numpy as jnp
from jax import lax
from jax.sharding import PartitionSpec as P


def short_conv(padded, taps):
    return taps[0] * padded[2:] + taps[1] * padded[1:-1] + taps[2] * padded[:-2]


def modal_long_conv(signal, rates, residues, skips):
    length, width = signal.shape
    order = rates.shape[0]
    ctx_count = lax.axis_size("ctx")
    coefs = residues * jnp.sqrt(2.0 * rates)
    times = jnp.arange(length, dtype=jnp.float32)[None, :, None]
    grow = jnp.exp(rates[:, None, :] * times)
    decay = jnp.exp(-rates[:, None, :] * times)
    lifted = grow * signal[None]
    rows = jnp.arange(length, dtype=jnp.int32)
    lower = (rows[:, None] >= rows[None, :]).astype(jnp.float32)
    lower = jnp.broadcast_to(lower[None], (order, length, length))
    running = lax.dot_general(
        lower,
        lifted,
        (((2,), (1,)), ((0,), (0,))),
        precision=lax.Precision.HIGHEST,
        preferred_element_type=jnp.float32,
    )
    end_state = running[:, length - 1] * jnp.exp(-rates * (length - 1))
    carried = jnp.zeros_like(end_state)
    for shift in range(1, ctx_count):
        earlier = lax.ppermute(
            end_state, "ctx", perm=[(i, i + shift) for i in range(ctx_count - shift)]
        )
        carried = carried + jnp.exp(-rates * (length * (shift - 1))) * earlier
    carried = carried * jnp.exp(-rates)
    total = running + carried[:, None, :]
    mixed = jnp.sum((coefs[:, None, :] * decay) * total, axis=0)
    return mixed + skips * signal


def ring_order(count):
    if count % 2:
        return list(range(count))
    return list(range(0, count, 2)) + list(range(count - 1, 0, -2))


def body(
    tokens,
    w_query,
    w_key,
    w_value,
    taps_query,
    taps_key,
    taps_value,
    decay_rate,
    residue,
    skip_gain,
    w_out,
):
    ctx_count = lax.axis_size("ctx")
    length = tokens.shape[0]
    width = w_query.shape[1]
    columns = lax.all_to_all(tokens, "ctx", split_axis=1, concat_axis=0, tiled=True)
    columns = jnp.concatenate([jnp.zeros((2, columns.shape[1]), columns.dtype), columns], axis=0)
    w_cat = jnp.concatenate([w_query, w_key, w_value], axis=1)
    split = w_cat.shape[1] // 2
    halves = (w_cat[:, :split], w_cat[:, split:])

    def piece(dest, side):
        rows = lax.dynamic_slice_in_dim(columns, dest * length, length + 2, 0)
        return jnp.dot(rows, halves[side], preferred_element_type=jnp.float32)

    ring = ring_order(ctx_count)
    place = [0] * ctx_count
    for pos, dev in enumerate(ring):
        place[dev] = pos
    fwd = [(ring[k], ring[(k + 1) % ctx_count]) for k in range(ctx_count)]
    bwd = [(ring[(k + 1) % ctx_count], ring[k]) for k in range(ctx_count)]
    me = lax.axis_index("ctx")
    my_pos = jnp.array(place, jnp.int32)[me]
    ring_arr = jnp.array(ring, jnp.int32)
    c_chunk = w_out.shape[0]
    c_half = c_chunk // 2
    w_up, w_low = w_out[:c_half], w_out[c_half:]
    w_rows = jnp.zeros((2 * ctx_count, c_half, w_out.shape[1]), w_out.dtype)
    w_rows = lax.dynamic_update_slice_in_dim(w_rows, w_up[None], me * 2, 0)
    w_rows = lax.dynamic_update_slice_in_dim(w_rows, w_low[None], me * 2 + 1, 0)

    def w_step(step, w_up, w_low, w_rows):
        src_up = ring_arr[(my_pos - step) % ctx_count]
        src_low = ring_arr[(my_pos + step) % ctx_count]
        w_rows = lax.dynamic_update_slice_in_dim(w_rows, w_up[None], src_up * 2, 0)
        return lax.dynamic_update_slice_in_dim(w_rows, w_low[None], src_low * 2 + 1, 0)

    early = min(3, ctx_count - 1)
    for step in range(1, early + 1):
        w_up = lax.ppermute(w_up, "ctx", perm=fwd)
        w_low = lax.ppermute(w_low, "ctx", perm=bwd)
        w_rows = w_step(step, w_up, w_low, w_rows)
    w_up, w_low, columns = lax.optimization_barrier((w_up, w_low, columns))
    up = piece(ring_arr[(my_pos - 1) % ctx_count], 0)
    down = piece(ring_arr[(my_pos + 1) % ctx_count], 1)
    for step in range(1, ctx_count):
        w_more = early + step < ctx_count
        if w_more:
            sent = lax.optimization_barrier(
                (up.astype(jnp.bfloat16), down.astype(jnp.bfloat16), w_up, w_low)
            )
            up, w_up = lax.ppermute((sent[0], sent[2]), "ctx", perm=fwd)
            down, w_low = lax.ppermute((sent[1], sent[3]), "ctx", perm=bwd)
            w_rows = w_step(early + step, w_up, w_low, w_rows)
        else:
            up = lax.ppermute(up.astype(jnp.bfloat16), "ctx", perm=fwd)
            down = lax.ppermute(down.astype(jnp.bfloat16), "ctx", perm=bwd)
        up = up.astype(jnp.float32) + piece(ring_arr[(my_pos - step - 1) % ctx_count], 0)
        down = down.astype(jnp.float32) + piece(ring_arr[(my_pos + step + 1) % ctx_count], 1)

    projected = jnp.concatenate([up, down], axis=1).astype(jnp.bfloat16).astype(jnp.float32)
    queries = projected[:, :width]
    keys_proj = projected[:, width : 2 * width]
    values_proj = projected[:, 2 * width :]
    gate = short_conv(queries, taps_query).astype(jnp.bfloat16)
    product = (short_conv(keys_proj, taps_key) * short_conv(values_proj, taps_value)).astype(
        jnp.bfloat16
    )
    mixed = modal_long_conv(product.astype(jnp.float32), decay_rate, residue, skip_gain)
    mixed = mixed.astype(jnp.bfloat16)
    gated = (gate.astype(jnp.float32) * mixed.astype(jnp.float32)).astype(jnp.bfloat16)
    features = lax.all_gather(gated, "tp", axis=1, tiled=True)
    w_full = w_rows.reshape(ctx_count * c_chunk, w_out.shape[1])
    result = jnp.dot(features, w_full, preferred_element_type=jnp.float32)
    return result.astype(jnp.bfloat16)


def solution(mesh):
    in_specs = (
        P("ctx", None),
        P("ctx", "tp"),
        P("ctx", "tp"),
        P("ctx", "tp"),
        P(None, "tp"),
        P(None, "tp"),
        P(None, "tp"),
        P(None, "tp"),
        P(None, "tp"),
        P("tp"),
        P("ctx", "tp"),
    )
    out_specs = P("ctx", "tp")
    return jax.shard_map(body, mesh=mesh, in_specs=in_specs, out_specs=out_specs, check_vma=False)
```

```python
import jax
import jax.numpy as jnp
from jax import lax
from jax.sharding import PartitionSpec as P


def short_conv(padded, taps):
    return taps[0] * padded[2:] + taps[1] * padded[1:-1] + taps[2] * padded[:-2]


def modal_long_conv(signal, rates, residues, skips):
    length, width = signal.shape
    order = rates.shape[0]
    ctx_count = lax.axis_size("ctx")
    coefs = residues * jnp.sqrt(2.0 * rates)
    times = jnp.arange(length, dtype=jnp.float32)[None, :, None]
    grow = jnp.exp(rates[:, None, :] * times)
    decay = jnp.exp(-rates[:, None, :] * times)
    lifted = grow * signal[None]
    rows = jnp.arange(length, dtype=jnp.int32)
    lower = (rows[:, None] >= rows[None, :]).astype(jnp.float32)
    lower = jnp.broadcast_to(lower[None], (order, length, length))
    running = lax.dot_general(
        lower,
        lifted,
        (((2,), (1,)), ((0,), (0,))),
        precision=lax.Precision.HIGHEST,
        preferred_element_type=jnp.float32,
    )
    end_state = running[:, length - 1] * jnp.exp(-rates * (length - 1))
    carried = jnp.zeros_like(end_state)
    for shift in range(1, ctx_count):
        earlier = lax.ppermute(
            end_state, "ctx", perm=[(i, i + shift) for i in range(ctx_count - shift)]
        )
        carried = carried + jnp.exp(-rates * (length * (shift - 1))) * earlier
    carried = carried * jnp.exp(-rates)
    total = running + carried[:, None, :]
    mixed = jnp.sum((coefs[:, None, :] * decay) * total, axis=0)
    return mixed + skips * signal


def ring_order(count):
    if count % 2:
        return list(range(count))
    return list(range(0, count, 2)) + list(range(count - 1, 0, -2))


def body(
    tokens,
    w_query,
    w_key,
    w_value,
    taps_query,
    taps_key,
    taps_value,
    decay_rate,
    residue,
    skip_gain,
    w_out,
):
    ctx_count = lax.axis_size("ctx")
    length = tokens.shape[0]
    width = w_query.shape[1]
    w_cat = jnp.concatenate([w_query, w_key, w_value], axis=1)
    split = w_cat.shape[1] // 2
    halves = (w_cat[:, :split], w_cat[:, split:])

    def piece(dest, side):
        rows = lax.dynamic_slice_in_dim(columns, dest * length, length + 2, 0)
        return jnp.dot(rows, halves[side], preferred_element_type=jnp.float32)

    ring = ring_order(ctx_count)
    place = [0] * ctx_count
    for pos, dev in enumerate(ring):
        place[dev] = pos
    fwd = [(ring[k], ring[(k + 1) % ctx_count]) for k in range(ctx_count)]
    bwd = [(ring[(k + 1) % ctx_count], ring[k]) for k in range(ctx_count)]
    me = lax.axis_index("ctx")
    my_pos = jnp.array(place, jnp.int32)[me]
    ring_arr = jnp.array(ring, jnp.int32)
    d_chunk = tokens.shape[1] // ctx_count
    blocks = jnp.zeros((ctx_count, length, d_chunk), tokens.dtype)
    blocks = lax.dynamic_update_slice_in_dim(
        blocks, lax.dynamic_slice_in_dim(tokens, me * d_chunk, d_chunk, 1)[None], me, 0
    )
    for offset in range(1, ctx_count):
        dest = ring_arr[(my_pos + offset) % ctx_count]
        src_dev = ring_arr[(my_pos - offset) % ctx_count]
        shift = [(ring[k], ring[(k + offset) % ctx_count]) for k in range(ctx_count)]
        outgoing = lax.dynamic_slice_in_dim(tokens, dest * d_chunk, d_chunk, 1)
        incoming = lax.ppermute(outgoing, "ctx", perm=shift)
        blocks = lax.dynamic_update_slice_in_dim(blocks, incoming[None], src_dev, 0)
    columns = blocks.reshape(ctx_count * length, d_chunk)
    columns = jnp.concatenate([jnp.zeros((2, d_chunk), columns.dtype), columns], axis=0)
    c_chunk = w_out.shape[0]
    c_half = c_chunk // 2
    w_up, w_low, columns = lax.optimization_barrier((w_out[:c_half], w_out[c_half:], columns))
    w_rows = jnp.zeros((2 * ctx_count, c_half, w_out.shape[1]), w_out.dtype)
    w_rows = lax.dynamic_update_slice_in_dim(w_rows, w_up[None], me * 2, 0)
    w_rows = lax.dynamic_update_slice_in_dim(w_rows, w_low[None], me * 2 + 1, 0)
    up = piece(ring_arr[(my_pos - 1) % ctx_count], 0)
    down = piece(ring_arr[(my_pos + 1) % ctx_count], 1)
    for step in range(1, ctx_count):
        sent = lax.optimization_barrier(
            (up.astype(jnp.bfloat16), down.astype(jnp.bfloat16), w_up, w_low)
        )
        up, w_up = lax.ppermute((sent[0], sent[2]), "ctx", perm=fwd)
        down, w_low = lax.ppermute((sent[1], sent[3]), "ctx", perm=bwd)
        src_up = ring_arr[(my_pos - step) % ctx_count]
        src_low = ring_arr[(my_pos + step) % ctx_count]
        w_rows = lax.dynamic_update_slice_in_dim(w_rows, w_up[None], src_up * 2, 0)
        w_rows = lax.dynamic_update_slice_in_dim(w_rows, w_low[None], src_low * 2 + 1, 0)
        up = up.astype(jnp.float32) + piece(ring_arr[(my_pos - step - 1) % ctx_count], 0)
        down = down.astype(jnp.float32) + piece(ring_arr[(my_pos + step + 1) % ctx_count], 1)

    projected = jnp.concatenate([up, down], axis=1).astype(jnp.bfloat16).astype(jnp.float32)
    queries = projected[:, :width]
    keys_proj = projected[:, width : 2 * width]
    values_proj = projected[:, 2 * width :]
    gate = short_conv(queries, taps_query).astype(jnp.bfloat16)
    product = (short_conv(keys_proj, taps_key) * short_conv(values_proj, taps_value)).astype(
        jnp.bfloat16
    )
    mixed = modal_long_conv(product.astype(jnp.float32), decay_rate, residue, skip_gain)
    mixed = mixed.astype(jnp.bfloat16)
    gated = (gate.astype(jnp.float32) * mixed.astype(jnp.float32)).astype(jnp.bfloat16)
    features = lax.all_gather(gated, "tp", axis=1, tiled=True)
    w_full = w_rows.reshape(ctx_count * c_chunk, w_out.shape[1])
    result = jnp.dot(features, w_full, preferred_element_type=jnp.float32)
    return result.astype(jnp.bfloat16)


def solution(mesh):
    in_specs = (
        P("ctx", None),
        P("ctx", "tp"),
        P("ctx", "tp"),
        P("ctx", "tp"),
        P(None, "tp"),
        P(None, "tp"),
        P(None, "tp"),
        P(None, "tp"),
        P(None, "tp"),
        P("tp"),
        P("ctx", "tp"),
    )
    out_specs = P("ctx", "tp")
    return jax.shard_map(body, mesh=mesh, in_specs=in_specs, out_specs=out_specs, check_vma=False)
```

```python
import jax
import jax.numpy as jnp
from jax import lax
from jax.sharding import PartitionSpec as P


def short_conv(padded, taps):
    return taps[0] * padded[2:] + taps[1] * padded[1:-1] + taps[2] * padded[:-2]


def modal_long_conv(signal, rates, residues, skips):
    length, width = signal.shape
    order = rates.shape[0]
    ctx_count = lax.axis_size("ctx")
    coefs = residues * jnp.sqrt(2.0 * rates)
    times = jnp.arange(length, dtype=jnp.float32)[None, :, None]
    grow = jnp.exp(rates[:, None, :] * times)
    decay = jnp.exp(-rates[:, None, :] * times)
    lifted = grow * signal[None]
    rows = jnp.arange(length, dtype=jnp.int32)
    lower = (rows[:, None] >= rows[None, :]).astype(jnp.float32)
    lower = jnp.broadcast_to(lower[None], (order, length, length))
    running = lax.dot_general(
        lower,
        lifted,
        (((2,), (1,)), ((0,), (0,))),
        precision=lax.Precision.HIGHEST,
        preferred_element_type=jnp.float32,
    )
    end_state = running[:, length - 1] * jnp.exp(-rates * (length - 1))
    carried = jnp.zeros_like(end_state)
    for shift in range(1, ctx_count):
        earlier = lax.ppermute(
            end_state, "ctx", perm=[(i, i + shift) for i in range(ctx_count - shift)]
        )
        carried = carried + jnp.exp(-rates * (length * (shift - 1))) * earlier
    carried = carried * jnp.exp(-rates)
    total = running + carried[:, None, :]
    mixed = jnp.sum((coefs[:, None, :] * decay) * total, axis=0)
    return mixed + skips * signal


def ring_order(count):
    if count % 2:
        return list(range(count))
    return list(range(0, count, 2)) + list(range(count - 1, 0, -2))


def body(
    tokens,
    w_query,
    w_key,
    w_value,
    taps_query,
    taps_key,
    taps_value,
    decay_rate,
    residue,
    skip_gain,
    w_out,
):
    ctx_count = lax.axis_size("ctx")
    length = tokens.shape[0]
    width = w_query.shape[1]
    by_dest = tokens.reshape(length, ctx_count, -1).transpose(1, 0, 2)
    columns = lax.all_to_all(by_dest, "ctx", split_axis=0, concat_axis=0, tiled=True)
    columns = columns.reshape(ctx_count * length, -1)
    columns = jnp.concatenate([jnp.zeros((2, columns.shape[1]), columns.dtype), columns], axis=0)
    w_cat = jnp.concatenate([w_query, w_key, w_value], axis=1)
    split = w_cat.shape[1] // 2
    halves = (w_cat[:, :split], w_cat[:, split:])

    def piece(dest, side):
        rows = lax.dynamic_slice_in_dim(columns, dest * length, length + 2, 0)
        return jnp.dot(rows, halves[side], preferred_element_type=jnp.float32)

    ring = ring_order(ctx_count)
    place = [0] * ctx_count
    for pos, dev in enumerate(ring):
        place[dev] = pos
    fwd = [(ring[k], ring[(k + 1) % ctx_count]) for k in range(ctx_count)]
    bwd = [(ring[(k + 1) % ctx_count], ring[k]) for k in range(ctx_count)]
    me = lax.axis_index("ctx")
    my_pos = jnp.array(place, jnp.int32)[me]
    ring_arr = jnp.array(ring, jnp.int32)
    c_chunk = w_out.shape[0]
    c_half = c_chunk // 2
    w_up, w_low, columns = lax.optimization_barrier((w_out[:c_half], w_out[c_half:], columns))
    w_rows = jnp.zeros((2 * ctx_count, c_half, w_out.shape[1]), w_out.dtype)
    w_rows = lax.dynamic_update_slice_in_dim(w_rows, w_up[None], me * 2, 0)
    w_rows = lax.dynamic_update_slice_in_dim(w_rows, w_low[None], me * 2 + 1, 0)

    def w_step(step, w_up, w_low, w_rows):
        src_up = ring_arr[(my_pos - step) % ctx_count]
        src_low = ring_arr[(my_pos + step) % ctx_count]
        w_rows = lax.dynamic_update_slice_in_dim(w_rows, w_up[None], src_up * 2, 0)
        return lax.dynamic_update_slice_in_dim(w_rows, w_low[None], src_low * 2 + 1, 0)

    up = piece(ring_arr[(my_pos - 1) % ctx_count], 0)
    down = piece(ring_arr[(my_pos + 1) % ctx_count], 1)
    tied = max(ctx_count - 3, 0)
    for step in range(1, ctx_count):
        if step <= tied:
            sent = lax.optimization_barrier(
                (up.astype(jnp.bfloat16), down.astype(jnp.bfloat16), w_up, w_low)
            )
            up, w_up = lax.ppermute((sent[0], sent[2]), "ctx", perm=fwd)
            down, w_low = lax.ppermute((sent[1], sent[3]), "ctx", perm=bwd)
            w_rows = w_step(step, w_up, w_low, w_rows)
        else:
            up = lax.ppermute(up.astype(jnp.bfloat16), "ctx", perm=fwd)
            down = lax.ppermute(down.astype(jnp.bfloat16), "ctx", perm=bwd)
        up = up.astype(jnp.float32) + piece(ring_arr[(my_pos - step - 1) % ctx_count], 0)
        down = down.astype(jnp.float32) + piece(ring_arr[(my_pos + step + 1) % ctx_count], 1)
    for step in range(tied + 1, ctx_count):
        w_up = lax.ppermute(w_up, "ctx", perm=fwd)
        w_low = lax.ppermute(w_low, "ctx", perm=bwd)
        w_rows = w_step(step, w_up, w_low, w_rows)

    projected = jnp.concatenate([up, down], axis=1).astype(jnp.bfloat16).astype(jnp.float32)
    queries = projected[:, :width]
    keys_proj = projected[:, width : 2 * width]
    values_proj = projected[:, 2 * width :]
    gate = short_conv(queries, taps_query).astype(jnp.bfloat16)
    product = (short_conv(keys_proj, taps_key) * short_conv(values_proj, taps_value)).astype(
        jnp.bfloat16
    )
    mixed = modal_long_conv(product.astype(jnp.float32), decay_rate, residue, skip_gain)
    mixed = mixed.astype(jnp.bfloat16)
    gated = (gate.astype(jnp.float32) * mixed.astype(jnp.float32)).astype(jnp.bfloat16)
    features = lax.all_gather(gated, "tp", axis=1, tiled=True)
    w_full = w_rows.reshape(ctx_count * c_chunk, w_out.shape[1])
    result = jnp.dot(features, w_full, preferred_element_type=jnp.float32)
    return result.astype(jnp.bfloat16)


def solution(mesh):
    in_specs = (
        P("ctx", None),
        P("ctx", "tp"),
        P("ctx", "tp"),
        P("ctx", "tp"),
        P(None, "tp"),
        P(None, "tp"),
        P(None, "tp"),
        P(None, "tp"),
        P(None, "tp"),
        P("tp"),
        P("ctx", "tp"),
    )
    out_specs = P("ctx", "tp")
    return jax.shard_map(body, mesh=mesh, in_specs=in_specs, out_specs=out_specs, check_vma=False)
```

```python
import jax
import jax.numpy as jnp
from jax import lax
from jax.sharding import PartitionSpec as P


def short_conv(padded, taps):
    return taps[0] * padded[2:] + taps[1] * padded[1:-1] + taps[2] * padded[:-2]


def modal_long_conv(signal, rates, residues, skips):
    length, width = signal.shape
    order = rates.shape[0]
    ctx_count = lax.axis_size("ctx")
    coefs = residues * jnp.sqrt(2.0 * rates)
    times = jnp.arange(length, dtype=jnp.float32)[None, :, None]
    grow = jnp.exp(rates[:, None, :] * times)
    decay = jnp.exp(-rates[:, None, :] * times)
    lifted = grow * signal[None]
    rows = jnp.arange(length, dtype=jnp.int32)
    lower = (rows[:, None] >= rows[None, :]).astype(jnp.float32)
    lower = jnp.broadcast_to(lower[None], (order, length, length))
    running = lax.dot_general(
        lower,
        lifted,
        (((2,), (1,)), ((0,), (0,))),
        precision=lax.Precision.HIGHEST,
        preferred_element_type=jnp.float32,
    )
    end_state = running[:, length - 1] * jnp.exp(-rates * (length - 1))
    carried = jnp.zeros_like(end_state)
    for shift in range(1, ctx_count):
        earlier = lax.ppermute(
            end_state, "ctx", perm=[(i, i + shift) for i in range(ctx_count - shift)]
        )
        carried = carried + jnp.exp(-rates * (length * (shift - 1))) * earlier
    carried = carried * jnp.exp(-rates)
    total = running + carried[:, None, :]
    mixed = jnp.sum((coefs[:, None, :] * decay) * total, axis=0)
    return mixed + skips * signal


def ring_order(count):
    if count % 2:
        return list(range(count))
    return list(range(0, count, 2)) + list(range(count - 1, 0, -2))


def body(
    tokens,
    w_query,
    w_key,
    w_value,
    taps_query,
    taps_key,
    taps_value,
    decay_rate,
    residue,
    skip_gain,
    w_out,
):
    ctx_count = lax.axis_size("ctx")
    length = tokens.shape[0]
    width = w_query.shape[1]
    by_dest = tokens.reshape(length, ctx_count, -1).transpose(1, 0, 2)
    columns = lax.all_to_all(by_dest, "ctx", split_axis=0, concat_axis=0, tiled=True)
    columns = columns.reshape(ctx_count * length, -1)
    columns = jnp.concatenate([jnp.zeros((2, columns.shape[1]), columns.dtype), columns], axis=0)
    w_cat = jnp.concatenate([w_query, w_key, w_value], axis=1)
    split = w_cat.shape[1] // 2
    halves = (w_cat[:, :split], w_cat[:, split:])

    def piece(dest, side):
        rows = lax.dynamic_slice_in_dim(columns, dest * length, length + 2, 0)
        return jnp.dot(rows, halves[side], preferred_element_type=jnp.float32)

    ring = ring_order(ctx_count)
    place = [0] * ctx_count
    for pos, dev in enumerate(ring):
        place[dev] = pos
    fwd = [(ring[k], ring[(k + 1) % ctx_count]) for k in range(ctx_count)]
    bwd = [(ring[(k + 1) % ctx_count], ring[k]) for k in range(ctx_count)]
    me = lax.axis_index("ctx")
    my_pos = jnp.array(place, jnp.int32)[me]
    ring_arr = jnp.array(ring, jnp.int32)
    c_chunk = w_out.shape[0]
    c_half = c_chunk // 2
    w_up, w_low, columns = lax.optimization_barrier((w_out[:c_half], w_out[c_half:], columns))
    w_rows = jnp.zeros((2 * ctx_count, c_half, w_out.shape[1]), w_out.dtype)
    w_rows = lax.dynamic_update_slice_in_dim(w_rows, w_up[None], me * 2, 0)
    w_rows = lax.dynamic_update_slice_in_dim(w_rows, w_low[None], me * 2 + 1, 0)

    def w_step(step, w_up, w_low, w_rows):
        src_up = ring_arr[(my_pos - step) % ctx_count]
        src_low = ring_arr[(my_pos + step) % ctx_count]
        w_rows = lax.dynamic_update_slice_in_dim(w_rows, w_up[None], src_up * 2, 0)
        return lax.dynamic_update_slice_in_dim(w_rows, w_low[None], src_low * 2 + 1, 0)

    up = piece(ring_arr[(my_pos - 1) % ctx_count], 0)
    down = piece(ring_arr[(my_pos + 1) % ctx_count], 1)
    tied = max(ctx_count - 4, 0)
    for step in range(1, ctx_count):
        if step <= tied:
            sent = lax.optimization_barrier(
                (up.astype(jnp.bfloat16), down.astype(jnp.bfloat16), w_up, w_low)
            )
            up, w_up = lax.ppermute((sent[0], sent[2]), "ctx", perm=fwd)
            down, w_low = lax.ppermute((sent[1], sent[3]), "ctx", perm=bwd)
            w_rows = w_step(step, w_up, w_low, w_rows)
        else:
            up = lax.ppermute(up.astype(jnp.bfloat16), "ctx", perm=fwd)
            down = lax.ppermute(down.astype(jnp.bfloat16), "ctx", perm=bwd)
        up = up.astype(jnp.float32) + piece(ring_arr[(my_pos - step - 1) % ctx_count], 0)
        down = down.astype(jnp.float32) + piece(ring_arr[(my_pos + step + 1) % ctx_count], 1)
    for step in range(tied + 1, ctx_count):
        w_up = lax.ppermute(w_up, "ctx", perm=fwd)
        w_low = lax.ppermute(w_low, "ctx", perm=bwd)
        w_rows = w_step(step, w_up, w_low, w_rows)

    projected = jnp.concatenate([up, down], axis=1).astype(jnp.bfloat16).astype(jnp.float32)
    queries = projected[:, :width]
    keys_proj = projected[:, width : 2 * width]
    values_proj = projected[:, 2 * width :]
    gate = short_conv(queries, taps_query).astype(jnp.bfloat16)
    product = (short_conv(keys_proj, taps_key) * short_conv(values_proj, taps_value)).astype(
        jnp.bfloat16
    )
    mixed = modal_long_conv(product.astype(jnp.float32), decay_rate, residue, skip_gain)
    mixed = mixed.astype(jnp.bfloat16)
    gated = (gate.astype(jnp.float32) * mixed.astype(jnp.float32)).astype(jnp.bfloat16)
    features = lax.all_gather(gated, "tp", axis=1, tiled=True)
    w_full = w_rows.reshape(ctx_count * c_chunk, w_out.shape[1])
    result = jnp.dot(features, w_full, preferred_element_type=jnp.float32)
    return result.astype(jnp.bfloat16)


def solution(mesh):
    in_specs = (
        P("ctx", None),
        P("ctx", "tp"),
        P("ctx", "tp"),
        P("ctx", "tp"),
        P(None, "tp"),
        P(None, "tp"),
        P(None, "tp"),
        P(None, "tp"),
        P(None, "tp"),
        P("tp"),
        P("ctx", "tp"),
    )
    out_specs = P("ctx", "tp")
    return jax.shard_map(body, mesh=mesh, in_specs=in_specs, out_specs=out_specs, check_vma=False)
```

```python
import jax
import jax.numpy as jnp
from jax import lax
from jax.sharding import PartitionSpec as P


def short_conv(padded, taps):
    return taps[0] * padded[2:] + taps[1] * padded[1:-1] + taps[2] * padded[:-2]


def modal_long_conv(signal, rates, residues, skips):
    length, width = signal.shape
    order = rates.shape[0]
    ctx_count = lax.axis_size("ctx")
    coefs = residues * jnp.sqrt(2.0 * rates)
    times = jnp.arange(length, dtype=jnp.float32)[None, :, None]
    grow = jnp.exp(rates[:, None, :] * times)
    decay = jnp.exp(-rates[:, None, :] * times)
    lifted = grow * signal[None]
    rows = jnp.arange(length, dtype=jnp.int32)
    lower = (rows[:, None] >= rows[None, :]).astype(jnp.float32)
    lower = jnp.broadcast_to(lower[None], (order, length, length))
    running = lax.dot_general(
        lower,
        lifted,
        (((2,), (1,)), ((0,), (0,))),
        precision=lax.Precision.HIGHEST,
        preferred_element_type=jnp.float32,
    )
    end_state = running[:, length - 1] * jnp.exp(-rates * (length - 1))
    me = lax.axis_index("ctx")
    later = jnp.arange(ctx_count, dtype=jnp.int32)
    gap = jnp.maximum(later - 1 - me, 0).astype(jnp.float32)
    sendable = jnp.where(
        (later > me)[:, None, None],
        jnp.exp(-rates[None] * (gap[:, None, None] * length)) * end_state[None],
        0.0,
    )
    received = lax.all_to_all(sendable, "ctx", split_axis=0, concat_axis=0, tiled=True)
    carried = jnp.sum(received, axis=0)
    carried = carried * jnp.exp(-rates)
    total = running + carried[:, None, :]
    mixed = jnp.sum((coefs[:, None, :] * decay) * total, axis=0)
    return mixed + skips * signal


def ring_order(count):
    if count % 2:
        return list(range(count))
    return list(range(0, count, 2)) + list(range(count - 1, 0, -2))


def body(
    tokens,
    w_query,
    w_key,
    w_value,
    taps_query,
    taps_key,
    taps_value,
    decay_rate,
    residue,
    skip_gain,
    w_out,
):
    ctx_count = lax.axis_size("ctx")
    length = tokens.shape[0]
    width = w_query.shape[1]
    by_dest = tokens.reshape(length, ctx_count, -1).transpose(1, 0, 2)
    columns = lax.all_to_all(by_dest, "ctx", split_axis=0, concat_axis=0, tiled=True)
    columns = columns.reshape(ctx_count * length, -1)
    columns = jnp.concatenate([jnp.zeros((2, columns.shape[1]), columns.dtype), columns], axis=0)
    w_cat = jnp.concatenate([w_query, w_key, w_value], axis=1)
    split = w_cat.shape[1] // 2
    halves = (w_cat[:, :split], w_cat[:, split:])

    def piece(dest, side):
        rows = lax.dynamic_slice_in_dim(columns, dest * length, length + 2, 0)
        return jnp.dot(rows, halves[side], preferred_element_type=jnp.float32)

    ring = ring_order(ctx_count)
    place = [0] * ctx_count
    for pos, dev in enumerate(ring):
        place[dev] = pos
    fwd = [(ring[k], ring[(k + 1) % ctx_count]) for k in range(ctx_count)]
    bwd = [(ring[(k + 1) % ctx_count], ring[k]) for k in range(ctx_count)]
    me = lax.axis_index("ctx")
    my_pos = jnp.array(place, jnp.int32)[me]
    ring_arr = jnp.array(ring, jnp.int32)
    c_chunk = w_out.shape[0]
    c_half = c_chunk // 2
    w_up, w_low, columns = lax.optimization_barrier((w_out[:c_half], w_out[c_half:], columns))
    w_rows = jnp.zeros((2 * ctx_count, c_half, w_out.shape[1]), w_out.dtype)
    w_rows = lax.dynamic_update_slice_in_dim(w_rows, w_up[None], me * 2, 0)
    w_rows = lax.dynamic_update_slice_in_dim(w_rows, w_low[None], me * 2 + 1, 0)

    def w_step(step, w_up, w_low, w_rows):
        src_up = ring_arr[(my_pos - step) % ctx_count]
        src_low = ring_arr[(my_pos + step) % ctx_count]
        w_rows = lax.dynamic_update_slice_in_dim(w_rows, w_up[None], src_up * 2, 0)
        return lax.dynamic_update_slice_in_dim(w_rows, w_low[None], src_low * 2 + 1, 0)

    up = piece(ring_arr[(my_pos - 1) % ctx_count], 0)
    down = piece(ring_arr[(my_pos + 1) % ctx_count], 1)
    tied = max(ctx_count - 4, 0)
    for step in range(1, ctx_count):
        if step <= tied:
            sent = lax.optimization_barrier(
                (up.astype(jnp.bfloat16), down.astype(jnp.bfloat16), w_up, w_low)
            )
            up, w_up = lax.ppermute((sent[0], sent[2]), "ctx", perm=fwd)
            down, w_low = lax.ppermute((sent[1], sent[3]), "ctx", perm=bwd)
            w_rows = w_step(step, w_up, w_low, w_rows)
        else:
            up = lax.ppermute(up.astype(jnp.bfloat16), "ctx", perm=fwd)
            down = lax.ppermute(down.astype(jnp.bfloat16), "ctx", perm=bwd)
        up = up.astype(jnp.float32) + piece(ring_arr[(my_pos - step - 1) % ctx_count], 0)
        down = down.astype(jnp.float32) + piece(ring_arr[(my_pos + step + 1) % ctx_count], 1)
    for step in range(tied + 1, ctx_count):
        w_up = lax.ppermute(w_up, "ctx", perm=fwd)
        w_low = lax.ppermute(w_low, "ctx", perm=bwd)
        w_rows = w_step(step, w_up, w_low, w_rows)

    projected = jnp.concatenate([up, down], axis=1).astype(jnp.bfloat16).astype(jnp.float32)
    queries = projected[:, :width]
    keys_proj = projected[:, width : 2 * width]
    values_proj = projected[:, 2 * width :]
    gate = short_conv(queries, taps_query).astype(jnp.bfloat16)
    product = (short_conv(keys_proj, taps_key) * short_conv(values_proj, taps_value)).astype(
        jnp.bfloat16
    )
    mixed = modal_long_conv(product.astype(jnp.float32), decay_rate, residue, skip_gain)
    mixed = mixed.astype(jnp.bfloat16)
    gated = (gate.astype(jnp.float32) * mixed.astype(jnp.float32)).astype(jnp.bfloat16)
    features = lax.all_gather(gated, "tp", axis=1, tiled=True)
    w_full = w_rows.reshape(ctx_count * c_chunk, w_out.shape[1])
    result = jnp.dot(features, w_full, preferred_element_type=jnp.float32)
    return result.astype(jnp.bfloat16)


def solution(mesh):
    in_specs = (
        P("ctx", None),
        P("ctx", "tp"),
        P("ctx", "tp"),
        P("ctx", "tp"),
        P(None, "tp"),
        P(None, "tp"),
        P(None, "tp"),
        P(None, "tp"),
        P(None, "tp"),
        P("tp"),
        P("ctx", "tp"),
    )
    out_specs = P("ctx", "tp")
    return jax.shard_map(body, mesh=mesh, in_specs=in_specs, out_specs=out_specs, check_vma=False)
```

```python
import jax
import jax.numpy as jnp
from jax import lax
from jax.sharding import PartitionSpec as P


def short_conv(padded, taps):
    return taps[0] * padded[2:] + taps[1] * padded[1:-1] + taps[2] * padded[:-2]


def modal_long_conv(signal, rates, residues, skips):
    length, width = signal.shape
    order = rates.shape[0]
    ctx_count = lax.axis_size("ctx")
    coefs = residues * jnp.sqrt(2.0 * rates)
    times = jnp.arange(length, dtype=jnp.float32)[None, :, None]
    grow = jnp.exp(rates[:, None, :] * times)
    decay = jnp.exp(-rates[:, None, :] * times)
    lifted = grow * signal[None]
    rows = jnp.arange(length, dtype=jnp.int32)
    lower = (rows[:, None] >= rows[None, :]).astype(jnp.float32)
    lower = jnp.broadcast_to(lower[None], (order, length, length))
    running = lax.dot_general(
        lower,
        lifted,
        (((2,), (1,)), ((0,), (0,))),
        precision=lax.Precision.HIGHEST,
        preferred_element_type=jnp.float32,
    )
    end_state = jnp.sum(lifted, axis=1) * jnp.exp(-rates * (length - 1))
    carried = jnp.zeros_like(end_state)
    for shift in range(1, ctx_count):
        earlier = lax.ppermute(
            end_state, "ctx", perm=[(i, i + shift) for i in range(ctx_count - shift)]
        )
        carried = carried + jnp.exp(-rates * (length * (shift - 1))) * earlier
    carried = carried * jnp.exp(-rates)
    total = running + carried[:, None, :]
    mixed = jnp.sum((coefs[:, None, :] * decay) * total, axis=0)
    return mixed + skips * signal


def ring_order(count):
    if count % 2:
        return list(range(count))
    return list(range(0, count, 2)) + list(range(count - 1, 0, -2))


def body(
    tokens,
    w_query,
    w_key,
    w_value,
    taps_query,
    taps_key,
    taps_value,
    decay_rate,
    residue,
    skip_gain,
    w_out,
):
    ctx_count = lax.axis_size("ctx")
    length = tokens.shape[0]
    width = w_query.shape[1]
    by_dest = tokens.reshape(length, ctx_count, -1).transpose(1, 0, 2)
    columns = lax.all_to_all(by_dest, "ctx", split_axis=0, concat_axis=0, tiled=True)
    columns = columns.reshape(ctx_count * length, -1)
    columns = jnp.concatenate([jnp.zeros((2, columns.shape[1]), columns.dtype), columns], axis=0)
    w_cat = jnp.concatenate([w_query, w_key, w_value], axis=1)
    split = w_cat.shape[1] // 2
    halves = (w_cat[:, :split], w_cat[:, split:])

    def piece(dest, side):
        rows = lax.dynamic_slice_in_dim(columns, dest * length, length + 2, 0)
        return jnp.dot(rows, halves[side], preferred_element_type=jnp.float32)

    ring = ring_order(ctx_count)
    place = [0] * ctx_count
    for pos, dev in enumerate(ring):
        place[dev] = pos
    fwd = [(ring[k], ring[(k + 1) % ctx_count]) for k in range(ctx_count)]
    bwd = [(ring[(k + 1) % ctx_count], ring[k]) for k in range(ctx_count)]
    me = lax.axis_index("ctx")
    my_pos = jnp.array(place, jnp.int32)[me]
    ring_arr = jnp.array(ring, jnp.int32)
    c_chunk = w_out.shape[0]
    c_half = c_chunk // 2
    w_up, w_low, columns = lax.optimization_barrier((w_out[:c_half], w_out[c_half:], columns))
    w_rows = jnp.zeros((2 * ctx_count, c_half, w_out.shape[1]), w_out.dtype)
    w_rows = lax.dynamic_update_slice_in_dim(w_rows, w_up[None], me * 2, 0)
    w_rows = lax.dynamic_update_slice_in_dim(w_rows, w_low[None], me * 2 + 1, 0)

    def w_step(step, w_up, w_low, w_rows):
        src_up = ring_arr[(my_pos - step) % ctx_count]
        src_low = ring_arr[(my_pos + step) % ctx_count]
        w_rows = lax.dynamic_update_slice_in_dim(w_rows, w_up[None], src_up * 2, 0)
        return lax.dynamic_update_slice_in_dim(w_rows, w_low[None], src_low * 2 + 1, 0)

    up = piece(ring_arr[(my_pos - 1) % ctx_count], 0)
    down = piece(ring_arr[(my_pos + 1) % ctx_count], 1)
    tied = max(ctx_count - 4, 0)
    for step in range(1, ctx_count):
        if step <= tied:
            sent = lax.optimization_barrier(
                (up.astype(jnp.bfloat16), down.astype(jnp.bfloat16), w_up, w_low)
            )
            up, w_up = lax.ppermute((sent[0], sent[2]), "ctx", perm=fwd)
            down, w_low = lax.ppermute((sent[1], sent[3]), "ctx", perm=bwd)
            w_rows = w_step(step, w_up, w_low, w_rows)
        else:
            up = lax.ppermute(up.astype(jnp.bfloat16), "ctx", perm=fwd)
            down = lax.ppermute(down.astype(jnp.bfloat16), "ctx", perm=bwd)
        up = up.astype(jnp.float32) + piece(ring_arr[(my_pos - step - 1) % ctx_count], 0)
        down = down.astype(jnp.float32) + piece(ring_arr[(my_pos + step + 1) % ctx_count], 1)
    for step in range(tied + 1, ctx_count):
        w_up = lax.ppermute(w_up, "ctx", perm=fwd)
        w_low = lax.ppermute(w_low, "ctx", perm=bwd)
        w_rows = w_step(step, w_up, w_low, w_rows)

    projected = jnp.concatenate([up, down], axis=1).astype(jnp.bfloat16).astype(jnp.float32)
    queries = projected[:, :width]
    keys_proj = projected[:, width : 2 * width]
    values_proj = projected[:, 2 * width :]
    gate = short_conv(queries, taps_query).astype(jnp.bfloat16)
    product = (short_conv(keys_proj, taps_key) * short_conv(values_proj, taps_value)).astype(
        jnp.bfloat16
    )
    mixed = modal_long_conv(product.astype(jnp.float32), decay_rate, residue, skip_gain)
    mixed = mixed.astype(jnp.bfloat16)
    gated = (gate.astype(jnp.float32) * mixed.astype(jnp.float32)).astype(jnp.bfloat16)
    features = lax.all_gather(gated, "tp", axis=1, tiled=True)
    w_full = w_rows.reshape(ctx_count * c_chunk, w_out.shape[1])
    result = jnp.dot(features, w_full, preferred_element_type=jnp.float32)
    return result.astype(jnp.bfloat16)


def solution(mesh):
    in_specs = (
        P("ctx", None),
        P("ctx", "tp"),
        P("ctx", "tp"),
        P("ctx", "tp"),
        P(None, "tp"),
        P(None, "tp"),
        P(None, "tp"),
        P(None, "tp"),
        P(None, "tp"),
        P("tp"),
        P("ctx", "tp"),
    )
    out_specs = P("ctx", "tp")
    return jax.shard_map(body, mesh=mesh, in_specs=in_specs, out_specs=out_specs, check_vma=False)
```

```python
import jax
import jax.numpy as jnp
from jax import lax
from jax.sharding import PartitionSpec as P


def short_conv(padded, taps):
    return taps[0] * padded[2:] + taps[1] * padded[1:-1] + taps[2] * padded[:-2]


def modal_long_conv(signal, rates, residues, skips):
    length, width = signal.shape
    order = rates.shape[0]
    ctx_count = lax.axis_size("ctx")
    coefs = residues * jnp.sqrt(2.0 * rates)
    times = jnp.arange(length, dtype=jnp.float32)[None, :, None]
    grow = jnp.exp(rates[:, None, :] * times)
    decay = jnp.exp(-rates[:, None, :] * times)
    lifted = grow * signal[None]
    rows = jnp.arange(length, dtype=jnp.int32)
    lower = (rows[:, None] >= rows[None, :]).astype(jnp.float32)
    lower = jnp.broadcast_to(lower[None], (order, length, length))
    running = lax.dot_general(
        lower,
        lifted,
        (((2,), (1,)), ((0,), (0,))),
        precision=lax.Precision.HIGH,
        preferred_element_type=jnp.float32,
    )
    end_state = jnp.sum(lifted, axis=1) * jnp.exp(-rates * (length - 1))
    carried = jnp.zeros_like(end_state)
    for shift in range(1, ctx_count):
        earlier = lax.ppermute(
            end_state, "ctx", perm=[(i, i + shift) for i in range(ctx_count - shift)]
        )
        carried = carried + jnp.exp(-rates * (length * (shift - 1))) * earlier
    carried = carried * jnp.exp(-rates)
    total = running + carried[:, None, :]
    mixed = jnp.sum((coefs[:, None, :] * decay) * total, axis=0)
    return mixed + skips * signal


def ring_order(count):
    if count % 2:
        return list(range(count))
    return list(range(0, count, 2)) + list(range(count - 1, 0, -2))


def body(
    tokens,
    w_query,
    w_key,
    w_value,
    taps_query,
    taps_key,
    taps_value,
    decay_rate,
    residue,
    skip_gain,
    w_out,
):
    ctx_count = lax.axis_size("ctx")
    length = tokens.shape[0]
    width = w_query.shape[1]
    by_dest = tokens.reshape(length, ctx_count, -1).transpose(1, 0, 2)
    columns = lax.all_to_all(by_dest, "ctx", split_axis=0, concat_axis=0, tiled=True)
    columns = columns.reshape(ctx_count * length, -1)
    columns = jnp.concatenate([jnp.zeros((2, columns.shape[1]), columns.dtype), columns], axis=0)
    w_cat = jnp.concatenate([w_query, w_key, w_value], axis=1)
    split = w_cat.shape[1] // 2
    halves = (w_cat[:, :split], w_cat[:, split:])

    def piece(dest, side):
        rows = lax.dynamic_slice_in_dim(columns, dest * length, length + 2, 0)
        return jnp.dot(rows, halves[side], preferred_element_type=jnp.float32)

    ring = ring_order(ctx_count)
    place = [0] * ctx_count
    for pos, dev in enumerate(ring):
        place[dev] = pos
    fwd = [(ring[k], ring[(k + 1) % ctx_count]) for k in range(ctx_count)]
    bwd = [(ring[(k + 1) % ctx_count], ring[k]) for k in range(ctx_count)]
    me = lax.axis_index("ctx")
    my_pos = jnp.array(place, jnp.int32)[me]
    ring_arr = jnp.array(ring, jnp.int32)
    c_chunk = w_out.shape[0]
    c_half = c_chunk // 2
    w_up, w_low, columns = lax.optimization_barrier((w_out[:c_half], w_out[c_half:], columns))
    w_rows = jnp.zeros((2 * ctx_count, c_half, w_out.shape[1]), w_out.dtype)
    w_rows = lax.dynamic_update_slice_in_dim(w_rows, w_up[None], me * 2, 0)
    w_rows = lax.dynamic_update_slice_in_dim(w_rows, w_low[None], me * 2 + 1, 0)

    def w_step(step, w_up, w_low, w_rows):
        src_up = ring_arr[(my_pos - step) % ctx_count]
        src_low = ring_arr[(my_pos + step) % ctx_count]
        w_rows = lax.dynamic_update_slice_in_dim(w_rows, w_up[None], src_up * 2, 0)
        return lax.dynamic_update_slice_in_dim(w_rows, w_low[None], src_low * 2 + 1, 0)

    up = piece(ring_arr[(my_pos - 1) % ctx_count], 0)
    down = piece(ring_arr[(my_pos + 1) % ctx_count], 1)
    tied = max(ctx_count - 4, 0)
    for step in range(1, ctx_count):
        if step <= tied:
            sent = lax.optimization_barrier(
                (up.astype(jnp.bfloat16), down.astype(jnp.bfloat16), w_up, w_low)
            )
            up, w_up = lax.ppermute((sent[0], sent[2]), "ctx", perm=fwd)
            down, w_low = lax.ppermute((sent[1], sent[3]), "ctx", perm=bwd)
            w_rows = w_step(step, w_up, w_low, w_rows)
        else:
            up = lax.ppermute(up.astype(jnp.bfloat16), "ctx", perm=fwd)
            down = lax.ppermute(down.astype(jnp.bfloat16), "ctx", perm=bwd)
        up = up.astype(jnp.float32) + piece(ring_arr[(my_pos - step - 1) % ctx_count], 0)
        down = down.astype(jnp.float32) + piece(ring_arr[(my_pos + step + 1) % ctx_count], 1)
    for step in range(tied + 1, ctx_count):
        w_up = lax.ppermute(w_up, "ctx", perm=fwd)
        w_low = lax.ppermute(w_low, "ctx", perm=bwd)
        w_rows = w_step(step, w_up, w_low, w_rows)

    projected = jnp.concatenate([up, down], axis=1).astype(jnp.bfloat16).astype(jnp.float32)
    queries = projected[:, :width]
    keys_proj = projected[:, width : 2 * width]
    values_proj = projected[:, 2 * width :]
    gate = short_conv(queries, taps_query).astype(jnp.bfloat16)
    product = (short_conv(keys_proj, taps_key) * short_conv(values_proj, taps_value)).astype(
        jnp.bfloat16
    )
    mixed = modal_long_conv(product.astype(jnp.float32), decay_rate, residue, skip_gain)
    mixed = mixed.astype(jnp.bfloat16)
    gated = (gate.astype(jnp.float32) * mixed.astype(jnp.float32)).astype(jnp.bfloat16)
    features = lax.all_gather(gated, "tp", axis=1, tiled=True)
    w_full = w_rows.reshape(ctx_count * c_chunk, w_out.shape[1])
    result = jnp.dot(features, w_full, preferred_element_type=jnp.float32)
    return result.astype(jnp.bfloat16)


def solution(mesh):
    in_specs = (
        P("ctx", None),
        P("ctx", "tp"),
        P("ctx", "tp"),
        P("ctx", "tp"),
        P(None, "tp"),
        P(None, "tp"),
        P(None, "tp"),
        P(None, "tp"),
        P(None, "tp"),
        P("tp"),
        P("ctx", "tp"),
    )
    out_specs = P("ctx", "tp")
    return jax.shard_map(body, mesh=mesh, in_specs=in_specs, out_specs=out_specs, check_vma=False)
```

```python
import jax
import jax.numpy as jnp
from jax import lax
from jax.sharding import PartitionSpec as P


def short_conv(padded, taps):
    return taps[0] * padded[2:] + taps[1] * padded[1:-1] + taps[2] * padded[:-2]


def modal_long_conv(signal, rates, residues, skips):
    length, width = signal.shape
    order = rates.shape[0]
    ctx_count = lax.axis_size("ctx")
    coefs = residues * jnp.sqrt(2.0 * rates)
    times = jnp.arange(length, dtype=jnp.float32)[None, :, None]
    grow = jnp.exp(rates[:, None, :] * times)
    decay = jnp.exp(-rates[:, None, :] * times)
    lifted = grow * signal[None]
    rows = jnp.arange(length, dtype=jnp.int32)
    lower = (rows[:, None] >= rows[None, :]).astype(jnp.bfloat16)
    lower = jnp.broadcast_to(lower[None], (order, length, length))
    lifted_hi = lifted.astype(jnp.bfloat16)
    lifted_lo = (lifted - lifted_hi.astype(jnp.float32)).astype(jnp.bfloat16)
    dims = (((2,), (1,)), ((0,), (0,)))
    running = lax.dot_general(
        lower, lifted_hi, dims, preferred_element_type=jnp.float32
    ) + lax.dot_general(lower, lifted_lo, dims, preferred_element_type=jnp.float32)
    end_state = jnp.sum(lifted, axis=1) * jnp.exp(-rates * (length - 1))
    carried = jnp.zeros_like(end_state)
    for shift in range(1, ctx_count):
        earlier = lax.ppermute(
            end_state, "ctx", perm=[(i, i + shift) for i in range(ctx_count - shift)]
        )
        carried = carried + jnp.exp(-rates * (length * (shift - 1))) * earlier
    carried = carried * jnp.exp(-rates)
    total = running + carried[:, None, :]
    mixed = jnp.sum((coefs[:, None, :] * decay) * total, axis=0)
    return mixed + skips * signal


def ring_order(count):
    if count % 2:
        return list(range(count))
    return list(range(0, count, 2)) + list(range(count - 1, 0, -2))


def body(
    tokens,
    w_query,
    w_key,
    w_value,
    taps_query,
    taps_key,
    taps_value,
    decay_rate,
    residue,
    skip_gain,
    w_out,
):
    ctx_count = lax.axis_size("ctx")
    length = tokens.shape[0]
    width = w_query.shape[1]
    by_dest = tokens.reshape(length, ctx_count, -1).transpose(1, 0, 2)
    columns = lax.all_to_all(by_dest, "ctx", split_axis=0, concat_axis=0, tiled=True)
    columns = columns.reshape(ctx_count * length, -1)
    columns = jnp.concatenate([jnp.zeros((2, columns.shape[1]), columns.dtype), columns], axis=0)
    w_cat = jnp.concatenate([w_query, w_key, w_value], axis=1)
    split = w_cat.shape[1] // 2
    halves = (w_cat[:, :split], w_cat[:, split:])

    def piece(dest, side):
        rows = lax.dynamic_slice_in_dim(columns, dest * length, length + 2, 0)
        return jnp.dot(rows, halves[side], preferred_element_type=jnp.float32)

    ring = ring_order(ctx_count)
    place = [0] * ctx_count
    for pos, dev in enumerate(ring):
        place[dev] = pos
    fwd = [(ring[k], ring[(k + 1) % ctx_count]) for k in range(ctx_count)]
    bwd = [(ring[(k + 1) % ctx_count], ring[k]) for k in range(ctx_count)]
    me = lax.axis_index("ctx")
    my_pos = jnp.array(place, jnp.int32)[me]
    ring_arr = jnp.array(ring, jnp.int32)
    c_chunk = w_out.shape[0]
    c_half = c_chunk // 2
    w_up, w_low, columns = lax.optimization_barrier((w_out[:c_half], w_out[c_half:], columns))
    w_rows = jnp.zeros((2 * ctx_count, c_half, w_out.shape[1]), w_out.dtype)
    w_rows = lax.dynamic_update_slice_in_dim(w_rows, w_up[None], me * 2, 0)
    w_rows = lax.dynamic_update_slice_in_dim(w_rows, w_low[None], me * 2 + 1, 0)

    def w_step(step, w_up, w_low, w_rows):
        src_up = ring_arr[(my_pos - step) % ctx_count]
        src_low = ring_arr[(my_pos + step) % ctx_count]
        w_rows = lax.dynamic_update_slice_in_dim(w_rows, w_up[None], src_up * 2, 0)
        return lax.dynamic_update_slice_in_dim(w_rows, w_low[None], src_low * 2 + 1, 0)

    up = piece(ring_arr[(my_pos - 1) % ctx_count], 0)
    down = piece(ring_arr[(my_pos + 1) % ctx_count], 1)
    tied = max(ctx_count - 4, 0)
    for step in range(1, ctx_count):
        if step <= tied:
            sent = lax.optimization_barrier(
                (up.astype(jnp.bfloat16), down.astype(jnp.bfloat16), w_up, w_low)
            )
            up, w_up = lax.ppermute((sent[0], sent[2]), "ctx", perm=fwd)
            down, w_low = lax.ppermute((sent[1], sent[3]), "ctx", perm=bwd)
            w_rows = w_step(step, w_up, w_low, w_rows)
        else:
            up = lax.ppermute(up.astype(jnp.bfloat16), "ctx", perm=fwd)
            down = lax.ppermute(down.astype(jnp.bfloat16), "ctx", perm=bwd)
        up = up.astype(jnp.float32) + piece(ring_arr[(my_pos - step - 1) % ctx_count], 0)
        down = down.astype(jnp.float32) + piece(ring_arr[(my_pos + step + 1) % ctx_count], 1)
    for step in range(tied + 1, ctx_count):
        w_up = lax.ppermute(w_up, "ctx", perm=fwd)
        w_low = lax.ppermute(w_low, "ctx", perm=bwd)
        w_rows = w_step(step, w_up, w_low, w_rows)

    projected = jnp.concatenate([up, down], axis=1).astype(jnp.bfloat16).astype(jnp.float32)
    queries = projected[:, :width]
    keys_proj = projected[:, width : 2 * width]
    values_proj = projected[:, 2 * width :]
    gate = short_conv(queries, taps_query).astype(jnp.bfloat16)
    product = (short_conv(keys_proj, taps_key) * short_conv(values_proj, taps_value)).astype(
        jnp.bfloat16
    )
    mixed = modal_long_conv(product.astype(jnp.float32), decay_rate, residue, skip_gain)
    mixed = mixed.astype(jnp.bfloat16)
    gated = (gate.astype(jnp.float32) * mixed.astype(jnp.float32)).astype(jnp.bfloat16)
    features = lax.all_gather(gated, "tp", axis=1, tiled=True)
    w_full = w_rows.reshape(ctx_count * c_chunk, w_out.shape[1])
    result = jnp.dot(features, w_full, preferred_element_type=jnp.float32)
    return result.astype(jnp.bfloat16)


def solution(mesh):
    in_specs = (
        P("ctx", None),
        P("ctx", "tp"),
        P("ctx", "tp"),
        P("ctx", "tp"),
        P(None, "tp"),
        P(None, "tp"),
        P(None, "tp"),
        P(None, "tp"),
        P(None, "tp"),
        P("tp"),
        P("ctx", "tp"),
    )
    out_specs = P("ctx", "tp")
    return jax.shard_map(body, mesh=mesh, in_specs=in_specs, out_specs=out_specs, check_vma=False)
```

```python
import jax
import jax.numpy as jnp
from jax import lax
from jax.sharding import PartitionSpec as P


def short_conv(padded, taps):
    return taps[0] * padded[2:] + taps[1] * padded[1:-1] + taps[2] * padded[:-2]


def modal_long_conv(signal, rates, residues, skips):
    length, width = signal.shape
    order = rates.shape[0]
    ctx_count = lax.axis_size("ctx")
    coefs = residues * jnp.sqrt(2.0 * rates)
    times = jnp.arange(length, dtype=jnp.float32)[None, :, None]
    grow = jnp.exp(rates[:, None, :] * times)
    decay = 1.0 / grow
    lifted = grow * signal[None]
    rows = jnp.arange(length, dtype=jnp.int32)
    lower = (rows[:, None] >= rows[None, :]).astype(jnp.float32)
    lower = jnp.broadcast_to(lower[None], (order, length, length))
    running = lax.dot_general(
        lower,
        lifted,
        (((2,), (1,)), ((0,), (0,))),
        precision=lax.Precision.HIGH,
        preferred_element_type=jnp.float32,
    )
    end_state = jnp.sum(lifted, axis=1) * jnp.exp(-rates * (length - 1))
    carried = jnp.zeros_like(end_state)
    for shift in range(1, ctx_count):
        earlier = lax.ppermute(
            end_state, "ctx", perm=[(i, i + shift) for i in range(ctx_count - shift)]
        )
        carried = carried + jnp.exp(-rates * (length * (shift - 1))) * earlier
    carried = carried * jnp.exp(-rates)
    total = running + carried[:, None, :]
    mixed = jnp.sum((coefs[:, None, :] * decay) * total, axis=0)
    return mixed + skips * signal


def ring_order(count):
    if count % 2:
        return list(range(count))
    return list(range(0, count, 2)) + list(range(count - 1, 0, -2))


def body(
    tokens,
    w_query,
    w_key,
    w_value,
    taps_query,
    taps_key,
    taps_value,
    decay_rate,
    residue,
    skip_gain,
    w_out,
):
    ctx_count = lax.axis_size("ctx")
    length = tokens.shape[0]
    width = w_query.shape[1]
    by_dest = tokens.reshape(length, ctx_count, -1).transpose(1, 0, 2)
    columns = lax.all_to_all(by_dest, "ctx", split_axis=0, concat_axis=0, tiled=True)
    columns = columns.reshape(ctx_count * length, -1)
    columns = jnp.concatenate([jnp.zeros((2, columns.shape[1]), columns.dtype), columns], axis=0)
    w_cat = jnp.concatenate([w_query, w_key, w_value], axis=1)
    split = w_cat.shape[1] // 2
    halves = (w_cat[:, :split], w_cat[:, split:])

    def piece(dest, side):
        rows = lax.dynamic_slice_in_dim(columns, dest * length, length + 2, 0)
        return jnp.dot(rows, halves[side], preferred_element_type=jnp.float32)

    ring = ring_order(ctx_count)
    place = [0] * ctx_count
    for pos, dev in enumerate(ring):
        place[dev] = pos
    fwd = [(ring[k], ring[(k + 1) % ctx_count]) for k in range(ctx_count)]
    bwd = [(ring[(k + 1) % ctx_count], ring[k]) for k in range(ctx_count)]
    me = lax.axis_index("ctx")
    my_pos = jnp.array(place, jnp.int32)[me]
    ring_arr = jnp.array(ring, jnp.int32)
    c_chunk = w_out.shape[0]
    c_half = c_chunk // 2
    w_up, w_low, columns = lax.optimization_barrier((w_out[:c_half], w_out[c_half:], columns))
    w_rows = jnp.zeros((2 * ctx_count, c_half, w_out.shape[1]), w_out.dtype)
    w_rows = lax.dynamic_update_slice_in_dim(w_rows, w_up[None], me * 2, 0)
    w_rows = lax.dynamic_update_slice_in_dim(w_rows, w_low[None], me * 2 + 1, 0)

    def w_step(step, w_up, w_low, w_rows):
        src_up = ring_arr[(my_pos - step) % ctx_count]
        src_low = ring_arr[(my_pos + step) % ctx_count]
        w_rows = lax.dynamic_update_slice_in_dim(w_rows, w_up[None], src_up * 2, 0)
        return lax.dynamic_update_slice_in_dim(w_rows, w_low[None], src_low * 2 + 1, 0)

    up = piece(ring_arr[(my_pos - 1) % ctx_count], 0)
    down = piece(ring_arr[(my_pos + 1) % ctx_count], 1)
    tied = max(ctx_count - 4, 0)
    for step in range(1, ctx_count):
        if step <= tied:
            sent = lax.optimization_barrier(
                (up.astype(jnp.bfloat16), down.astype(jnp.bfloat16), w_up, w_low)
            )
            up, w_up = lax.ppermute((sent[0], sent[2]), "ctx", perm=fwd)
            down, w_low = lax.ppermute((sent[1], sent[3]), "ctx", perm=bwd)
            w_rows = w_step(step, w_up, w_low, w_rows)
        else:
            up = lax.ppermute(up.astype(jnp.bfloat16), "ctx", perm=fwd)
            down = lax.ppermute(down.astype(jnp.bfloat16), "ctx", perm=bwd)
        up = up.astype(jnp.float32) + piece(ring_arr[(my_pos - step - 1) % ctx_count], 0)
        down = down.astype(jnp.float32) + piece(ring_arr[(my_pos + step + 1) % ctx_count], 1)
    for step in range(tied + 1, ctx_count):
        w_up = lax.ppermute(w_up, "ctx", perm=fwd)
        w_low = lax.ppermute(w_low, "ctx", perm=bwd)
        w_rows = w_step(step, w_up, w_low, w_rows)

    projected = jnp.concatenate([up, down], axis=1).astype(jnp.bfloat16).astype(jnp.float32)
    queries = projected[:, :width]
    keys_proj = projected[:, width : 2 * width]
    values_proj = projected[:, 2 * width :]
    gate = short_conv(queries, taps_query).astype(jnp.bfloat16)
    product = (short_conv(keys_proj, taps_key) * short_conv(values_proj, taps_value)).astype(
        jnp.bfloat16
    )
    mixed = modal_long_conv(product.astype(jnp.float32), decay_rate, residue, skip_gain)
    mixed = mixed.astype(jnp.bfloat16)
    gated = (gate.astype(jnp.float32) * mixed.astype(jnp.float32)).astype(jnp.bfloat16)
    features = lax.all_gather(gated, "tp", axis=1, tiled=True)
    w_full = w_rows.reshape(ctx_count * c_chunk, w_out.shape[1])
    result = jnp.dot(features, w_full, preferred_element_type=jnp.float32)
    return result.astype(jnp.bfloat16)


def solution(mesh):
    in_specs = (
        P("ctx", None),
        P("ctx", "tp"),
        P("ctx", "tp"),
        P("ctx", "tp"),
        P(None, "tp"),
        P(None, "tp"),
        P(None, "tp"),
        P(None, "tp"),
        P(None, "tp"),
        P("tp"),
        P("ctx", "tp"),
    )
    out_specs = P("ctx", "tp")
    return jax.shard_map(body, mesh=mesh, in_specs=in_specs, out_specs=out_specs, check_vma=False)
```

```python
import jax
import jax.numpy as jnp
from jax import lax
from jax.sharding import PartitionSpec as P


def short_conv(padded, taps):
    return taps[0] * padded[2:] + taps[1] * padded[1:-1] + taps[2] * padded[:-2]


def modal_long_conv(signal, rates, residues, skips):
    length, width = signal.shape
    order = rates.shape[0]
    ctx_count = lax.axis_size("ctx")
    coefs = residues * jnp.sqrt(2.0 * rates)
    times = jnp.arange(length, dtype=jnp.float32)[None, :, None]
    grow = jnp.exp(rates[:, None, :] * times)
    decay = jnp.exp(-rates[:, None, :] * times)
    lifted = grow * signal[None]
    rows = jnp.arange(length, dtype=jnp.int32)
    lower = (rows[:, None] >= rows[None, :]).astype(jnp.float32)
    lower = jnp.broadcast_to(lower[None], (order, length, length))
    running = lax.dot_general(
        lower,
        lifted,
        (((2,), (1,)), ((0,), (0,))),
        precision=lax.Precision.HIGH,
        preferred_element_type=jnp.float32,
    )
    end_state = jnp.sum(lifted, axis=1) * jnp.exp(-rates * (length - 1))
    carried = jnp.zeros_like(end_state)
    for shift in range(1, ctx_count):
        earlier = lax.ppermute(
            end_state, "ctx", perm=[(i, i + shift) for i in range(ctx_count - shift)]
        )
        carried = carried + jnp.exp(-rates * (length * (shift - 1))) * earlier
    carried = carried * jnp.exp(-rates)
    total = running + carried[:, None, :]
    mixed = jnp.sum((coefs[:, None, :] * decay) * total, axis=0)
    return mixed + skips * signal


def ring_order(count):
    if count % 2:
        return list(range(count))
    return list(range(0, count, 2)) + list(range(count - 1, 0, -2))


def body(
    tokens,
    w_query,
    w_key,
    w_value,
    taps_query,
    taps_key,
    taps_value,
    decay_rate,
    residue,
    skip_gain,
    w_out,
):
    ctx_count = lax.axis_size("ctx")
    length = tokens.shape[0]
    width = w_query.shape[1]
    by_dest = tokens.reshape(length, ctx_count, -1).transpose(1, 0, 2)
    columns = lax.all_to_all(by_dest, "ctx", split_axis=0, concat_axis=0, tiled=True)
    columns = columns.reshape(ctx_count * length, -1)
    columns = jnp.concatenate([jnp.zeros((2, columns.shape[1]), columns.dtype), columns], axis=0)
    w_cat = jnp.concatenate([w_query, w_key, w_value], axis=1)
    split = w_cat.shape[1] // 2
    halves = (w_cat[:, :split], w_cat[:, split:])

    def piece(dest, side):
        rows = lax.dynamic_slice_in_dim(columns, dest * length, length + 2, 0)
        return jnp.dot(rows, halves[side], preferred_element_type=jnp.float32)

    ring = ring_order(ctx_count)
    place = [0] * ctx_count
    for pos, dev in enumerate(ring):
        place[dev] = pos
    fwd = [(ring[k], ring[(k + 1) % ctx_count]) for k in range(ctx_count)]
    bwd = [(ring[(k + 1) % ctx_count], ring[k]) for k in range(ctx_count)]
    me = lax.axis_index("ctx")
    my_pos = jnp.array(place, jnp.int32)[me]
    ring_arr = jnp.array(ring, jnp.int32)
    c_chunk = w_out.shape[0]
    c_half = c_chunk // 2
    w_up, w_low, columns = lax.optimization_barrier((w_out[:c_half], w_out[c_half:], columns))
    w_rows = jnp.zeros((2 * ctx_count, c_half, w_out.shape[1]), w_out.dtype)
    w_rows = lax.dynamic_update_slice_in_dim(w_rows, w_up[None], me * 2, 0)
    w_rows = lax.dynamic_update_slice_in_dim(w_rows, w_low[None], me * 2 + 1, 0)

    def w_step(step, w_up, w_low, w_rows):
        src_up = ring_arr[(my_pos - step) % ctx_count]
        src_low = ring_arr[(my_pos + step) % ctx_count]
        w_rows = lax.dynamic_update_slice_in_dim(w_rows, w_up[None], src_up * 2, 0)
        return lax.dynamic_update_slice_in_dim(w_rows, w_low[None], src_low * 2 + 1, 0)

    up = piece(ring_arr[(my_pos - 1) % ctx_count], 0)
    down = piece(ring_arr[(my_pos + 1) % ctx_count], 1)
    tied = max(ctx_count - 5, 0)
    for step in range(1, ctx_count):
        if step <= tied:
            sent = lax.optimization_barrier(
                (up.astype(jnp.bfloat16), down.astype(jnp.bfloat16), w_up, w_low)
            )
            up, w_up = lax.ppermute((sent[0], sent[2]), "ctx", perm=fwd)
            down, w_low = lax.ppermute((sent[1], sent[3]), "ctx", perm=bwd)
            w_rows = w_step(step, w_up, w_low, w_rows)
        else:
            up = lax.ppermute(up.astype(jnp.bfloat16), "ctx", perm=fwd)
            down = lax.ppermute(down.astype(jnp.bfloat16), "ctx", perm=bwd)
        up = up.astype(jnp.float32) + piece(ring_arr[(my_pos - step - 1) % ctx_count], 0)
        down = down.astype(jnp.float32) + piece(ring_arr[(my_pos + step + 1) % ctx_count], 1)
    for step in range(tied + 1, ctx_count):
        w_up = lax.ppermute(w_up, "ctx", perm=fwd)
        w_low = lax.ppermute(w_low, "ctx", perm=bwd)
        w_rows = w_step(step, w_up, w_low, w_rows)

    projected = jnp.concatenate([up, down], axis=1).astype(jnp.bfloat16).astype(jnp.float32)
    queries = projected[:, :width]
    keys_proj = projected[:, width : 2 * width]
    values_proj = projected[:, 2 * width :]
    gate = short_conv(queries, taps_query).astype(jnp.bfloat16)
    product = (short_conv(keys_proj, taps_key) * short_conv(values_proj, taps_value)).astype(
        jnp.bfloat16
    )
    mixed = modal_long_conv(product.astype(jnp.float32), decay_rate, residue, skip_gain)
    mixed = mixed.astype(jnp.bfloat16)
    gated = (gate.astype(jnp.float32) * mixed.astype(jnp.float32)).astype(jnp.bfloat16)
    features = lax.all_gather(gated, "tp", axis=1, tiled=True)
    w_full = w_rows.reshape(ctx_count * c_chunk, w_out.shape[1])
    result = jnp.dot(features, w_full, preferred_element_type=jnp.float32)
    return result.astype(jnp.bfloat16)


def solution(mesh):
    in_specs = (
        P("ctx", None),
        P("ctx", "tp"),
        P("ctx", "tp"),
        P("ctx", "tp"),
        P(None, "tp"),
        P(None, "tp"),
        P(None, "tp"),
        P(None, "tp"),
        P(None, "tp"),
        P("tp"),
        P("ctx", "tp"),
    )
    out_specs = P("ctx", "tp")
    return jax.shard_map(body, mesh=mesh, in_specs=in_specs, out_specs=out_specs, check_vma=False)
```
